512 devices in a mesh: section: 32 (over z, core), blk: 16 (over y, x).
Axes of the slice: x: 4, y: 4, z: 16, core: 2. Of those that a mesh axis runs over, the one named last changes fastest.
Arguments:
- held_input: bfloat16 [32, 5120, 128], P('section', 'blk'), may hold values from -6 to 6
- fresh_input: bfloat16 [5120, 128], P('blk'), may hold values from -6 to 6
- stashed: bfloat16 [32, 2, 5120, 128], P('section', None, 'blk'), may hold values from -6 to 6
- held_grad: bfloat16 [32, 5120, 128], P('section', 'blk'), may hold values from -6 to 6
- fresh_grad: bfloat16 [5120, 128], P('blk'), may hold values from -6 to 6
- first_up: bfloat16 [32, 2, 128, 6400], P('section', None, 'blk'), may hold values from -1 to 1
- second_up: bfloat16 [32, 2, 160, 16384], P('section', None, 'blk'), may hold values from -0.5 to 0.5
- first_down: bfloat16 [32, 160, 16384], P('section', 'blk'), may hold values from -0.5 to 0.5
- second_down: bfloat16 [32, 128, 6400], P('section', 'blk'), may hold values from -0.5 to 0.5
Outputs:
- passed_output: bfloat16 [32, 5120, 128], P('section', 'blk')
- passed_grad: bfloat16 [32, 5120, 128], P('section', 'blk')
- grad_first_up: bfloat16 [32, 2, 128, 6400], P('section', None, 'blk')
- grad_second_up: bfloat16 [32, 2, 160, 16384], P('section', None, 'blk')
- grad_first_down: bfloat16 [32, 160, 16384], P('section', 'blk')
- grad_second_down: bfloat16 [32, 128, 6400], P('section', 'blk')
The draws below stay inside these ranges and needn't reach their ends.
All inputs are finite; a program needn't handle non-finite values.
Results may differ from the reference program's by a relative error of at most 0.0095.
Values may be sent and summed in bfloat16 or wider, within the bound.
No kernel may reach another device: no remote copies, remote signals or barrier semaphores. Data moves between devices by JAX's collectives and lax.ppermute only.
A program may use at most 64 MiB of HBM per device.

```python
import math
import jax
import jax.numpy as jnp
from jax import lax

D = 5120
BLOCK = 128
FIRST_BLOCKS = 128
FIRST_IN = 40
SECOND_BLOCKS = 160
MB_TOK = 128
TICKS = 2
N_SECTION = 32


def levels(own_key, dims, shards, smallest, largest):
    loudness = 1.0
    for axis_at, shards_of in shards:
        heights = jax.random.uniform(jax.random.fold_in(jax.random.fold_in(own_key, 6), axis_at), (shards_of,), jnp.float32, smallest / len(shards), largest / len(shards))
        loudness = loudness * jnp.repeat(jnp.exp(heights), dims[axis_at] // shards_of).reshape((-1,) + (1,) * (len(dims) - 1 - axis_at))
    return loudness


def noise(own_key, dims, deviation, most, split=(), held_as=jnp.bfloat16):
    array = deviation * jax.random.normal(own_key, dims, jnp.float32)
    if split:
        array = array * levels(own_key, dims, split, -0.22, 0.18)
    return jnp.clip(array, -most, most).astype(held_as)


def setup_inputs(seed: int = 0) -> dict:
    arg_keys = jax.random.split(jax.random.key(seed), 10)
    held_input = noise(arg_keys[0], (N_SECTION, D, MB_TOK), 1.0, 6.0, ((0, 32), (1, 16)))
    fresh_input = noise(arg_keys[1], (D, MB_TOK), 1.0, 6.0, ((0, 16),))
    stashed = noise(arg_keys[2], (N_SECTION, TICKS, D, MB_TOK), 1.0, 6.0, ((0, 32), (2, 16)))
    held_grad = noise(arg_keys[3], (N_SECTION, D, MB_TOK), 1.0, 6.0, ((0, 32), (1, 16)))
    fresh_grad = noise(arg_keys[4], (D, MB_TOK), 1.0, 6.0, ((0, 16),))
    first_up = noise(arg_keys[5], (N_SECTION, 2, FIRST_BLOCKS, FIRST_IN * SECOND_BLOCKS), FIRST_IN ** -0.5, 1.0, ((0, 32), (2, 16)))
    second_up = noise(arg_keys[6], (N_SECTION, 2, SECOND_BLOCKS, FIRST_BLOCKS * BLOCK), FIRST_BLOCKS ** -0.5, 0.5, ((0, 32), (2, 16)))
    first_down = noise(arg_keys[7], (N_SECTION, SECOND_BLOCKS, BLOCK * FIRST_BLOCKS), BLOCK ** -0.5, 0.5, ((0, 32), (1, 16)))
    second_down = noise(arg_keys[8], (N_SECTION, FIRST_BLOCKS, SECOND_BLOCKS * FIRST_IN), SECOND_BLOCKS ** -0.5, 0.5, ((0, 32), (1, 16)))
    return dict(held_input=held_input, fresh_input=fresh_input, stashed=stashed, held_grad=held_grad, fresh_grad=fresh_grad, first_up=first_up, second_up=second_up, first_down=first_down, second_down=second_down)


def layer_tick(inputs, cotangent, stash, first_up, second_up, first_down, second_down):
    tokens = inputs.shape[1]
    up_first = first_up.reshape(2, FIRST_BLOCKS, FIRST_IN, SECOND_BLOCKS).astype(jnp.float32)
    up_second = second_up.reshape(2, SECOND_BLOCKS, FIRST_BLOCKS, BLOCK).astype(jnp.float32)
    down_first = first_down.reshape(SECOND_BLOCKS, BLOCK, FIRST_BLOCKS).astype(jnp.float32)
    down_second = second_down.reshape(FIRST_BLOCKS, SECOND_BLOCKS, FIRST_IN).astype(jnp.float32)

    def forward(source):
        values = source.reshape(FIRST_BLOCKS, FIRST_IN, tokens).astype(jnp.float32)
        spread = jnp.einsum('pqt,gpqr->gprt', values, up_first).astype(jnp.bfloat16)
        mixed = jnp.einsum('gprt,grpo->grot', spread.astype(jnp.float32), up_second)
        hidden = (jax.nn.silu(mixed[0]) * mixed[1]).astype(jnp.bfloat16)
        lowered = jnp.einsum('rot,rop->rpt', hidden.astype(jnp.float32), down_first).astype(jnp.bfloat16)
        result = values + jnp.einsum('rpt,prq->pqt', lowered.astype(jnp.float32), down_second)
        return (values, spread, mixed, hidden, lowered, result.astype(jnp.bfloat16))
    produced = forward(inputs)[5].reshape(D, tokens)
    values, spread, mixed, hidden, lowered, unused = forward(stash)
    grads = cotangent.reshape(FIRST_BLOCKS, FIRST_IN, tokens).astype(jnp.float32)
    grad_lowered = jnp.einsum('pqt,prq->prt', grads, down_second).astype(jnp.bfloat16)
    grad_hidden = jnp.einsum('prt,rop->rot', grad_lowered.astype(jnp.float32), down_first)
    sigmoid_gate = jax.nn.sigmoid(mixed[0])
    slope = sigmoid_gate * (1.0 + mixed[0] * (1.0 - sigmoid_gate))
    grad_mixed = jnp.stack([grad_hidden * mixed[1] * slope, grad_hidden * mixed[0] * sigmoid_gate]).astype(jnp.bfloat16)
    grad_spread = jnp.einsum('grot,grpo->grpt', grad_mixed.astype(jnp.float32), up_second).astype(jnp.bfloat16)
    back = grads + jnp.einsum('grpt,gpqr->pqt', grad_spread.astype(jnp.float32), up_first)
    term_first_up = jnp.einsum('pqt,grpt->gpqr', values, grad_spread.astype(jnp.float32))
    term_second_up = jnp.einsum('gprt,grot->grpo', spread.astype(jnp.float32), grad_mixed.astype(jnp.float32))
    term_first_down = jnp.einsum('rot,prt->rop', hidden.astype(jnp.float32), grad_lowered.astype(jnp.float32))
    term_second_down = jnp.einsum('rpt,pqt->prq', lowered.astype(jnp.float32), grads)
    return (produced, back.astype(jnp.bfloat16).reshape(D, tokens), term_first_up.reshape(first_up.shape), term_second_up.reshape(second_up.shape), term_first_down.reshape(first_down.shape), term_second_down.reshape(second_down.shape))

def one_section(operands):
    return layer_tick(operands[0], operands[1], operands[2], operands[3], operands[4], operands[5], operands[6])

def reference(held_input, fresh_input, stashed, held_grad, fresh_grad, first_up, second_up, first_down, second_down):
    inputs = held_input
    cotangent = held_grad
    totals = [jnp.zeros(weight.shape, jnp.float32) for weight in (first_up, second_up, first_down, second_down)]
    outputs = held_input
    backward = held_grad
    for tick_index in range(TICKS):
        results = lax.map(one_section, (inputs, cotangent, stashed[:, tick_index], first_up, second_up, first_down, second_down))
        outputs = results[0]
        backward = results[1]
        totals = [totals[number] + results[number + 2] for number in range(4)]
        if tick_index + 1 < TICKS:
            inputs = jnp.concatenate([fresh_input[None], outputs[:-1]], axis=0)
            cotangent = jnp.concatenate([backward[1:], fresh_grad[None]], axis=0)
    factor = 1.0 / math.sqrt(TICKS * MB_TOK)
    return (outputs, backward, (totals[0] * factor).astype(jnp.bfloat16), (totals[1] * factor).astype(jnp.bfloat16), (totals[2] * factor).astype(jnp.bfloat16), (totals[3] * factor).astype(jnp.bfloat16))
```

```python
import math

import jax
import jax.numpy as jnp
from jax import lax
from jax.sharding import PartitionSpec as P

BLOCK = 128
FIRST_BLOCKS = 128
FIRST_IN = 40
SECOND_BLOCKS = 160
TICKS = 2


def from_behind(value, axis, by):
    length = lax.axis_size(axis)
    pairs = [(i, i + by) for i in range(length) if 0 <= i + by < length]
    return lax.ppermute(value, axis, pairs)


def to_blocks(pieces):
    return lax.all_to_all(pieces, "blk", split_axis=1, concat_axis=0, tiled=True)


def to_features(pieces):
    return lax.all_to_all(pieces, "blk", split_axis=1, concat_axis=0, tiled=True)


def spread_of(values, up_first):
    return jnp.einsum(
        "pqt,gpqr->prgt", values, up_first, preferred_element_type=jnp.float32
    ).astype(jnp.bfloat16)


def lowered_grad_of(grads, down_second):
    return jnp.einsum(
        "pqt,prq->prt", grads, down_second, preferred_element_type=jnp.float32
    ).astype(jnp.bfloat16)


def forward_middle(spread_r, up_second, down_first):
    mixed = jnp.einsum(
        "prgt,grpo->grot", spread_r, up_second, preferred_element_type=jnp.float32
    )
    hidden = (jax.nn.silu(mixed[0]) * mixed[1]).astype(jnp.bfloat16)
    lowered = jnp.einsum(
        "rot,rop->rpt", hidden, down_first, preferred_element_type=jnp.float32
    ).astype(jnp.bfloat16)
    return mixed, hidden, lowered


def backward_middle(mixed, grad_lowered_r, up_second, down_first):
    grad_hidden = jnp.einsum(
        "prt,rop->rot", grad_lowered_r, down_first, preferred_element_type=jnp.float32
    )
    sigmoid_gate = jax.nn.sigmoid(mixed[0])
    slope = sigmoid_gate * (1.0 + mixed[0] * (1.0 - sigmoid_gate))
    grad_mixed = jnp.stack(
        [grad_hidden * mixed[1] * slope, grad_hidden * mixed[0] * sigmoid_gate]
    ).astype(jnp.bfloat16)
    grad_spread = jnp.einsum(
        "grot,grpo->rpgt", grad_mixed, up_second, preferred_element_type=jnp.float32
    ).astype(jnp.bfloat16)
    return grad_mixed, grad_spread


def output_of(values, lowered_p, down_second):
    added = jnp.einsum("rpt,prq->pqt", lowered_p, down_second, preferred_element_type=jnp.float32)
    return (values.astype(jnp.float32) + added).astype(jnp.bfloat16)


def input_grad_of(grads, grad_spread_p, up_first):
    added = jnp.einsum(
        "rpgt,gpqr->pqt", grad_spread_p, up_first, preferred_element_type=jnp.float32
    )
    return (grads.astype(jnp.float32) + added).astype(jnp.bfloat16)


def shards(
    held_input,
    fresh_input,
    stashed,
    held_grad,
    fresh_grad,
    first_up,
    second_up,
    first_down,
    second_down,
):
    feature_blocks = first_up.shape[2]
    hidden_blocks = second_up.shape[2]
    tokens = held_input.shape[2]
    up_first = first_up[0].reshape(2, feature_blocks, FIRST_IN, SECOND_BLOCKS)
    up_second = second_up[0].reshape(2, hidden_blocks, FIRST_BLOCKS, BLOCK)
    down_first = first_down[0].reshape(hidden_blocks, BLOCK, FIRST_BLOCKS)
    down_second = second_down[0].reshape(feature_blocks, SECOND_BLOCKS, FIRST_IN)
    first_inputs = held_input[0].reshape(feature_blocks, FIRST_IN, tokens)
    first_grads = held_grad[0].reshape(feature_blocks, FIRST_IN, tokens)
    stash_views = [
        stashed[0, k].reshape(feature_blocks, FIRST_IN, tokens) for k in range(TICKS)
    ]
    section_pos = lax.axis_index("section")
    last_section = lax.axis_size("section") - 1
    t = tokens

    values_a = jnp.concatenate([first_inputs] + stash_views, axis=2)
    spread_a = spread_of(values_a, up_first)
    glow_1 = lowered_grad_of(first_grads, down_second)
    payload = jnp.concatenate(
        [spread_a.reshape(feature_blocks, SECOND_BLOCKS, 2 * 3 * t), glow_1], axis=2
    )
    arrived = to_blocks(payload)
    spread_ar = arrived[:, :, : 6 * t].reshape(FIRST_BLOCKS, hidden_blocks, 2, 3 * t)
    glow_1r = arrived[:, :, 6 * t :]
    mixed_a, hidden_a, lowered_a = forward_middle(spread_ar, up_second, down_first)
    gmix_1, gspread_1 = backward_middle(mixed_a[:, :, :, t : 2 * t], glow_1r, up_second, down_first)
    payload = jnp.concatenate(
        [lowered_a, gspread_1.reshape(hidden_blocks, FIRST_BLOCKS, 2 * t)], axis=2
    )
    back = to_features(payload)
    lowered_ap = back[:, :, : 3 * t]
    gspread_1p = back[:, :, 3 * t :].reshape(SECOND_BLOCKS, feature_blocks, 2, t)
    outputs = output_of(first_inputs, lowered_ap[:, :, :t], down_second)
    backward = input_grad_of(first_grads, gspread_1p, up_first)

    moved_forward = from_behind(outputs, "section", 1)
    inputs = jnp.where(
        section_pos == 0,
        fresh_input.reshape(feature_blocks, FIRST_IN, tokens),
        moved_forward,
    )
    moved_backward = from_behind(backward, "section", -1)
    grads = jnp.where(
        section_pos == last_section,
        fresh_grad.reshape(feature_blocks, FIRST_IN, tokens),
        moved_backward,
    )

    spread_b = spread_of(inputs, up_first)
    glow_2 = lowered_grad_of(grads, down_second)
    payload = jnp.concatenate(
        [spread_b.reshape(feature_blocks, SECOND_BLOCKS, 2 * t), glow_2], axis=2
    )
    arrived = to_blocks(payload)
    spread_br = arrived[:, :, : 2 * t].reshape(FIRST_BLOCKS, hidden_blocks, 2, t)
    glow_2r = arrived[:, :, 2 * t :]
    _, _, lowered_b = forward_middle(spread_br, up_second, down_first)
    gmix_2, gspread_2 = backward_middle(
        mixed_a[:, :, :, 2 * t :], glow_2r, up_second, down_first
    )
    payload = jnp.concatenate(
        [lowered_b, gspread_2.reshape(hidden_blocks, FIRST_BLOCKS, 2 * t)], axis=2
    )
    back = to_features(payload)
    lowered_bp = back[:, :, :t]
    gspread_2p = back[:, :, t:].reshape(SECOND_BLOCKS, feature_blocks, 2, t)
    outputs = output_of(inputs, lowered_bp, down_second)
    backward = input_grad_of(grads, gspread_2p, up_first)

    stash_both = jnp.concatenate(stash_views, axis=2)
    gspread_both = jnp.concatenate([gspread_1p, gspread_2p], axis=3)
    spread_both = spread_ar[:, :, :, t:]
    gmix_both = jnp.concatenate([gmix_1, gmix_2], axis=3)
    hidden_both = hidden_a[:, :, t:]
    glow_both = jnp.concatenate([glow_1r, glow_2r], axis=2)
    lowered_both = lowered_ap[:, :, t:]
    grads_both = jnp.concatenate([first_grads, grads], axis=2)
    total_first_up = jnp.einsum(
        "pqt,rpgt->gpqr", stash_both, gspread_both, preferred_element_type=jnp.float32
    )
    total_second_up = jnp.einsum(
        "prgt,grot->grpo", spread_both, gmix_both, preferred_element_type=jnp.float32
    )
    total_first_down = jnp.einsum(
        "rot,prt->rop", hidden_both, glow_both, preferred_element_type=jnp.float32
    )
    total_second_down = jnp.einsum(
        "rpt,pqt->prq", lowered_both, grads_both, preferred_element_type=jnp.float32
    )
    factor = 1.0 / math.sqrt(TICKS * tokens)
    return (
        outputs.reshape(held_input.shape),
        backward.reshape(held_grad.shape),
        (total_first_up * factor).astype(jnp.bfloat16).reshape(first_up.shape),
        (total_second_up * factor).astype(jnp.bfloat16).reshape(second_up.shape),
        (total_first_down * factor).astype(jnp.bfloat16).reshape(first_down.shape),
        (total_second_down * factor).astype(jnp.bfloat16).reshape(second_down.shape),
    )


def solution(mesh):
    return jax.shard_map(
        shards,
        mesh=mesh,
        in_specs=(
            P("section", "blk", None),
            P("blk", None),
            P("section", None, "blk", None),
            P("section", "blk", None),
            P("blk", None),
            P("section", None, "blk", None),
            P("section", None, "blk", None),
            P("section", "blk", None),
            P("section", "blk", None),
        ),
        out_specs=(
            P("section", "blk", None),
            P("section", "blk", None),
            P("section", None, "blk", None),
            P("section", None, "blk", None),
            P("section", "blk", None),
            P("section", "blk", None),
        ),
        check_vma=False,
    )
```

```python
import math

import jax
import jax.numpy as jnp
from jax import lax
from jax.sharding import PartitionSpec as P

BLOCK = 128
FIRST_BLOCKS = 128
FIRST_IN = 40
SECOND_BLOCKS = 160
TICKS = 2


def from_behind(value, axis, by):
    length = lax.axis_size(axis)
    pairs = [(i, i + by) for i in range(length) if 0 <= i + by < length]
    return lax.ppermute(value, axis, pairs)


def exchange(pieces):
    return lax.all_to_all(pieces, "blk", split_axis=0, concat_axis=1, tiled=True)


def spread_of(values, up_first):
    spread = jnp.einsum(
        "pqt,gpqr->rpgt", values, up_first, preferred_element_type=jnp.float32
    ).astype(jnp.bfloat16)
    return spread.reshape(spread.shape[0], spread.shape[1], -1)


def lowered_grad_of(grads, down_second):
    return jnp.einsum(
        "pqt,prq->rpt", grads, down_second, preferred_element_type=jnp.float32
    ).astype(jnp.bfloat16)


def forward_middle(spread_r, up_second, down_first):
    mixed = jnp.einsum(
        "rpgt,grpo->grot", spread_r, up_second, preferred_element_type=jnp.float32
    )
    hidden = (jax.nn.silu(mixed[0]) * mixed[1]).astype(jnp.bfloat16)
    lowered = jnp.einsum(
        "rot,rop->prt", hidden, down_first, preferred_element_type=jnp.float32
    ).astype(jnp.bfloat16)
    return mixed, hidden, lowered


def backward_middle(mixed, grad_lowered_r, up_second, down_first):
    grad_hidden = jnp.einsum(
        "rpt,rop->rot", grad_lowered_r, down_first, preferred_element_type=jnp.float32
    )
    sigmoid_gate = jax.nn.sigmoid(mixed[0])
    slope = sigmoid_gate * (1.0 + mixed[0] * (1.0 - sigmoid_gate))
    grad_mixed = jnp.stack(
        [grad_hidden * mixed[1] * slope, grad_hidden * mixed[0] * sigmoid_gate]
    ).astype(jnp.bfloat16)
    grad_spread = jnp.einsum(
        "grot,grpo->prgt", grad_mixed, up_second, preferred_element_type=jnp.float32
    ).astype(jnp.bfloat16)
    return grad_mixed, grad_spread.reshape(grad_spread.shape[0], grad_spread.shape[1], -1)


def output_of(values, lowered_p, down_second):
    added = jnp.einsum("prt,prq->pqt", lowered_p, down_second, preferred_element_type=jnp.float32)
    return (values.astype(jnp.float32) + added).astype(jnp.bfloat16)


def input_grad_of(grads, grad_spread_p, up_first):
    added = jnp.einsum(
        "prgt,gpqr->pqt", grad_spread_p, up_first, preferred_element_type=jnp.float32
    )
    return (grads.astype(jnp.float32) + added).astype(jnp.bfloat16)


def shards(
    held_input,
    fresh_input,
    stashed,
    held_grad,
    fresh_grad,
    first_up,
    second_up,
    first_down,
    second_down,
):
    pb = first_up.shape[2]
    rb = second_up.shape[2]
    t = held_input.shape[2]
    up_first = first_up[0].reshape(2, pb, FIRST_IN, SECOND_BLOCKS)
    up_second = second_up[0].reshape(2, rb, FIRST_BLOCKS, BLOCK)
    down_first = first_down[0].reshape(rb, BLOCK, FIRST_BLOCKS)
    down_second = second_down[0].reshape(pb, SECOND_BLOCKS, FIRST_IN)
    first_inputs = held_input[0].reshape(pb, FIRST_IN, t)
    first_grads = held_grad[0].reshape(pb, FIRST_IN, t)
    stash_0 = stashed[0, 0].reshape(pb, FIRST_IN, t)
    stash_1 = stashed[0, 1].reshape(pb, FIRST_IN, t)
    section_pos = lax.axis_index("section")
    last_section = lax.axis_size("section") - 1

    spread_a = spread_of(jnp.concatenate([first_inputs, stash_0], axis=2), up_first)
    glow_1 = lowered_grad_of(first_grads, down_second)
    arrived = exchange(jnp.concatenate([spread_a, glow_1], axis=2))
    spread_ar = arrived[:, :, : 4 * t].reshape(rb, FIRST_BLOCKS, 2, 2 * t)
    glow_1r = arrived[:, :, 4 * t :]
    spread_s1r = exchange(spread_of(stash_1, up_first)).reshape(rb, FIRST_BLOCKS, 2, t)

    mixed_a, hidden_a, lowered_a = forward_middle(spread_ar, up_second, down_first)
    gmix_1, gspread_1 = backward_middle(mixed_a[..., t:], glow_1r, up_second, down_first)
    back = exchange(jnp.concatenate([lowered_a[..., :t], gspread_1], axis=2))
    outputs = output_of(first_inputs, back[..., :t], down_second)
    gspread_1p = back[..., t:].reshape(pb, SECOND_BLOCKS, 2, t)
    backward = input_grad_of(first_grads, gspread_1p, up_first)

    mixed_s1, hidden_s1, lowered_s1 = forward_middle(spread_s1r, up_second, down_first)
    lowered_sp = exchange(jnp.concatenate([lowered_a[..., t:], lowered_s1], axis=2))

    moved_forward = from_behind(outputs, "section", 1)
    inputs = jnp.where(section_pos == 0, fresh_input.reshape(pb, FIRST_IN, t), moved_forward)
    moved_backward = from_behind(backward, "section", -1)
    grads = jnp.where(
        section_pos == last_section, fresh_grad.reshape(pb, FIRST_IN, t), moved_backward
    )

    spread_b = spread_of(inputs, up_first)
    glow_2 = lowered_grad_of(grads, down_second)
    arrived = exchange(jnp.concatenate([spread_b, glow_2], axis=2))
    spread_br = arrived[:, :, : 2 * t].reshape(rb, FIRST_BLOCKS, 2, t)
    glow_2r = arrived[:, :, 2 * t :]
    _, _, lowered_b = forward_middle(spread_br, up_second, down_first)
    gmix_2, gspread_2 = backward_middle(mixed_s1, glow_2r, up_second, down_first)
    back = exchange(jnp.concatenate([lowered_b, gspread_2], axis=2))
    outputs = output_of(inputs, back[..., :t], down_second)
    gspread_2p = back[..., t:].reshape(pb, SECOND_BLOCKS, 2, t)
    backward = input_grad_of(grads, gspread_2p, up_first)

    stash_both = jnp.concatenate([stash_0, stash_1], axis=2)
    gspread_both = jnp.concatenate([gspread_1p, gspread_2p], axis=3)
    spread_both = jnp.concatenate([spread_ar[..., t:], spread_s1r], axis=3)
    gmix_both = jnp.concatenate([gmix_1, gmix_2], axis=3)
    hidden_both = jnp.concatenate([hidden_a[..., t:], hidden_s1], axis=2)
    glow_both = jnp.concatenate([glow_1r, glow_2r], axis=2)
    grads_both = jnp.concatenate([first_grads, grads], axis=2)
    total_first_up = jnp.einsum(
        "pqt,prgt->gpqr", stash_both, gspread_both, preferred_element_type=jnp.float32
    )
    total_second_up = jnp.einsum(
        "rpgt,grot->grpo", spread_both, gmix_both, preferred_element_type=jnp.float32
    )
    total_first_down = jnp.einsum(
        "rot,rpt->rop", hidden_both, glow_both, preferred_element_type=jnp.float32
    )
    total_second_down = jnp.einsum(
        "prt,pqt->prq", lowered_sp, grads_both, preferred_element_type=jnp.float32
    )
    factor = 1.0 / math.sqrt(TICKS * t)
    return (
        outputs.reshape(held_input.shape),
        backward.reshape(held_grad.shape),
        (total_first_up * factor).astype(jnp.bfloat16).reshape(first_up.shape),
        (total_second_up * factor).astype(jnp.bfloat16).reshape(second_up.shape),
        (total_first_down * factor).astype(jnp.bfloat16).reshape(first_down.shape),
        (total_second_down * factor).astype(jnp.bfloat16).reshape(second_down.shape),
    )


def solution(mesh):
    return jax.shard_map(
        shards,
        mesh=mesh,
        in_specs=(
            P("section", "blk", None),
            P("blk", None),
            P("section", None, "blk", None),
            P("section", "blk", None),
            P("blk", None),
            P("section", None, "blk", None),
            P("section", None, "blk", None),
            P("section", "blk", None),
            P("section", "blk", None),
        ),
        out_specs=(
            P("section", "blk", None),
            P("section", "blk", None),
            P("section", None, "blk", None),
            P("section", None, "blk", None),
            P("section", "blk", None),
            P("section", "blk", None),
        ),
        check_vma=False,
    )
```

```python
import math

import jax
import jax.numpy as jnp
from jax import lax
from jax.sharding import PartitionSpec as P

BLOCK = 128
FIRST_BLOCKS = 128
FIRST_IN = 40
SECOND_BLOCKS = 160
TICKS = 2


def from_behind(value, axis, by):
    length = lax.axis_size(axis)
    pairs = [(i, i + by) for i in range(length) if 0 <= i + by < length]
    return lax.ppermute(value, axis, pairs)


def to_blocks(pieces):
    return lax.all_to_all(pieces, "blk", split_axis=1, concat_axis=0, tiled=True)


def to_features(pieces):
    groups = lax.axis_size("blk")
    r_local, p_all, n = pieces.shape
    p_local = p_all // groups
    grouped = pieces.reshape(r_local, groups, p_local, n).transpose(1, 0, 2, 3)
    arrived = lax.all_to_all(grouped, "blk", split_axis=0, concat_axis=0, tiled=True)
    return arrived.reshape(groups * r_local, p_local, n)


def spread_of(values, up_first):
    return jnp.einsum(
        "pqt,gpqr->prgt", values, up_first, preferred_element_type=jnp.float32
    ).astype(jnp.bfloat16)


def lowered_grad_of(grads, down_second):
    return jnp.einsum(
        "pqt,prq->prt", grads, down_second, preferred_element_type=jnp.float32
    ).astype(jnp.bfloat16)


def forward_middle(spread_r, up_second, down_first):
    mixed = jnp.einsum(
        "prgt,grpo->grot", spread_r, up_second, preferred_element_type=jnp.float32
    )
    hidden = (jax.nn.silu(mixed[0]) * mixed[1]).astype(jnp.bfloat16)
    lowered = jnp.einsum(
        "rot,rop->rpt", hidden, down_first, preferred_element_type=jnp.float32
    ).astype(jnp.bfloat16)
    return mixed, hidden, lowered


def backward_middle(mixed, grad_lowered_r, up_second, down_first):
    grad_hidden = jnp.einsum(
        "prt,rop->rot", grad_lowered_r, down_first, preferred_element_type=jnp.float32
    )
    sigmoid_gate = jax.nn.sigmoid(mixed[0])
    slope = sigmoid_gate * (1.0 + mixed[0] * (1.0 - sigmoid_gate))
    grad_mixed = jnp.stack(
        [grad_hidden * mixed[1] * slope, grad_hidden * mixed[0] * sigmoid_gate]
    ).astype(jnp.bfloat16)
    grad_spread = jnp.einsum(
        "grot,grpo->rpgt", grad_mixed, up_second, preferred_element_type=jnp.float32
    ).astype(jnp.bfloat16)
    return grad_mixed, grad_spread


def output_of(values, lowered_p, down_second):
    added = jnp.einsum("rpt,prq->pqt", lowered_p, down_second, preferred_element_type=jnp.float32)
    return (values.astype(jnp.float32) + added).astype(jnp.bfloat16)


def input_grad_of(grads, grad_spread_p, up_first):
    added = jnp.einsum(
        "rpgt,gpqr->pqt", grad_spread_p, up_first, preferred_element_type=jnp.float32
    )
    return (grads.astype(jnp.float32) + added).astype(jnp.bfloat16)


def shards(
    held_input,
    fresh_input,
    stashed,
    held_grad,
    fresh_grad,
    first_up,
    second_up,
    first_down,
    second_down,
):
    feature_blocks = first_up.shape[2]
    hidden_blocks = second_up.shape[2]
    tokens = held_input.shape[2]
    up_first = first_up[0].reshape(2, feature_blocks, FIRST_IN, SECOND_BLOCKS)
    up_second = second_up[0].reshape(2, hidden_blocks, FIRST_BLOCKS, BLOCK)
    down_first = first_down[0].reshape(hidden_blocks, BLOCK, FIRST_BLOCKS)
    down_second = second_down[0].reshape(feature_blocks, SECOND_BLOCKS, FIRST_IN)
    first_inputs = held_input[0].reshape(feature_blocks, FIRST_IN, tokens)
    first_grads = held_grad[0].reshape(feature_blocks, FIRST_IN, tokens)
    stash_views = [
        stashed[0, k].reshape(feature_blocks, FIRST_IN, tokens) for k in range(TICKS)
    ]
    section_pos = lax.axis_index("section")
    last_section = lax.axis_size("section") - 1
    t = tokens

    values_a = jnp.concatenate([first_inputs] + stash_views, axis=2)
    spread_a = spread_of(values_a, up_first)
    glow_1 = lowered_grad_of(first_grads, down_second)
    payload = jnp.concatenate(
        [spread_a.reshape(feature_blocks, SECOND_BLOCKS, 2 * 3 * t), glow_1], axis=2
    )
    arrived = to_blocks(payload)
    spread_ar = arrived[:, :, : 6 * t].reshape(FIRST_BLOCKS, hidden_blocks, 2, 3 * t)
    glow_1r = arrived[:, :, 6 * t :]
    mixed_a, hidden_a, lowered_a = forward_middle(spread_ar, up_second, down_first)
    gmix_1, gspread_1 = backward_middle(mixed_a[:, :, :, t : 2 * t], glow_1r, up_second, down_first)
    payload = jnp.concatenate(
        [lowered_a, gspread_1.reshape(hidden_blocks, FIRST_BLOCKS, 2 * t)], axis=2
    )
    back = to_features(payload)
    lowered_ap = back[:, :, : 3 * t]
    gspread_1p = back[:, :, 3 * t :].reshape(SECOND_BLOCKS, feature_blocks, 2, t)
    outputs = output_of(first_inputs, lowered_ap[:, :, :t], down_second)
    backward = input_grad_of(first_grads, gspread_1p, up_first)

    moved_forward = from_behind(outputs, "section", 1)
    inputs = jnp.where(
        section_pos == 0,
        fresh_input.reshape(feature_blocks, FIRST_IN, tokens),
        moved_forward,
    )
    moved_backward = from_behind(backward, "section", -1)
    grads = jnp.where(
        section_pos == last_section,
        fresh_grad.reshape(feature_blocks, FIRST_IN, tokens),
        moved_backward,
    )

    spread_b = spread_of(inputs, up_first)
    glow_2 = lowered_grad_of(grads, down_second)
    payload = jnp.concatenate(
        [spread_b.reshape(feature_blocks, SECOND_BLOCKS, 2 * t), glow_2], axis=2
    )
    arrived = to_blocks(payload)
    spread_br = arrived[:, :, : 2 * t].reshape(FIRST_BLOCKS, hidden_blocks, 2, t)
    glow_2r = arrived[:, :, 2 * t :]
    _, _, lowered_b = forward_middle(spread_br, up_second, down_first)
    gmix_2, gspread_2 = backward_middle(
        mixed_a[:, :, :, 2 * t :], glow_2r, up_second, down_first
    )
    payload = jnp.concatenate(
        [lowered_b, gspread_2.reshape(hidden_blocks, FIRST_BLOCKS, 2 * t)], axis=2
    )
    back = to_features(payload)
    lowered_bp = back[:, :, :t]
    gspread_2p = back[:, :, t:].reshape(SECOND_BLOCKS, feature_blocks, 2, t)
    outputs = output_of(inputs, lowered_bp, down_second)
    backward = input_grad_of(grads, gspread_2p, up_first)

    stash_both = jnp.concatenate(stash_views, axis=2)
    gspread_both = jnp.concatenate([gspread_1p, gspread_2p], axis=3)
    spread_both = spread_ar[:, :, :, t:]
    gmix_both = jnp.concatenate([gmix_1, gmix_2], axis=3)
    hidden_both = hidden_a[:, :, t:]
    glow_both = jnp.concatenate([glow_1r, glow_2r], axis=2)
    lowered_both = lowered_ap[:, :, t:]
    grads_both = jnp.concatenate([first_grads, grads], axis=2)
    total_first_up = jnp.einsum(
        "pqt,rpgt->gpqr", stash_both, gspread_both, preferred_element_type=jnp.float32
    )
    total_second_up = jnp.einsum(
        "prgt,grot->grpo", spread_both, gmix_both, preferred_element_type=jnp.float32
    )
    total_first_down = jnp.einsum(
        "rot,prt->rop", hidden_both, glow_both, preferred_element_type=jnp.float32
    )
    total_second_down = jnp.einsum(
        "rpt,pqt->prq", lowered_both, grads_both, preferred_element_type=jnp.float32
    )
    factor = 1.0 / math.sqrt(TICKS * tokens)
    return (
        outputs.reshape(held_input.shape),
        backward.reshape(held_grad.shape),
        (total_first_up * factor).astype(jnp.bfloat16).reshape(first_up.shape),
        (total_second_up * factor).astype(jnp.bfloat16).reshape(second_up.shape),
        (total_first_down * factor).astype(jnp.bfloat16).reshape(first_down.shape),
        (total_second_down * factor).astype(jnp.bfloat16).reshape(second_down.shape),
    )


def solution(mesh):
    return jax.shard_map(
        shards,
        mesh=mesh,
        in_specs=(
            P("section", "blk", None),
            P("blk", None),
            P("section", None, "blk", None),
            P("section", "blk", None),
            P("blk", None),
            P("section", None, "blk", None),
            P("section", None, "blk", None),
            P("section", "blk", None),
            P("section", "blk", None),
        ),
        out_specs=(
            P("section", "blk", None),
            P("section", "blk", None),
            P("section", None, "blk", None),
            P("section", None, "blk", None),
            P("section", "blk", None),
            P("section", "blk", None),
        ),
        check_vma=False,
    )
```

```python
import math

import jax
import jax.numpy as jnp
from jax import lax
from jax.sharding import PartitionSpec as P

BLOCK = 128
FIRST_BLOCKS = 128
FIRST_IN = 40
SECOND_BLOCKS = 160
TICKS = 2


def from_behind(value, axis, by):
    length = lax.axis_size(axis)
    pairs = [(i, i + by) for i in range(length) if 0 <= i + by < length]
    return lax.ppermute(value, axis, pairs)


def to_blocks(pieces):
    return lax.all_to_all(pieces, "blk", split_axis=1, concat_axis=0, tiled=True)


def to_features(pieces):
    groups = lax.axis_size("blk")
    r_local, p_all, n = pieces.shape
    p_local = p_all // groups
    grouped = pieces.reshape(r_local, groups, p_local, n).transpose(1, 0, 2, 3)
    arrived = lax.all_to_all(grouped, "blk", split_axis=0, concat_axis=0, tiled=True)
    return arrived.reshape(groups * r_local, p_local, n)


def spread_of(values, up_first):
    return jnp.einsum(
        "pqt,gpqr->prgt", values, up_first, preferred_element_type=jnp.float32
    ).astype(jnp.bfloat16)


def lowered_grad_of(grads, down_second):
    return jnp.einsum(
        "pqt,prq->prt", grads, down_second, preferred_element_type=jnp.float32
    ).astype(jnp.bfloat16)


def forward_middle(spread_r, up_second, down_first):
    mixed = jnp.einsum(
        "prgt,grpo->grot", spread_r, up_second, preferred_element_type=jnp.float32
    )
    hidden = (jax.nn.silu(mixed[0]) * mixed[1]).astype(jnp.bfloat16)
    lowered = jnp.einsum(
        "rot,rop->rpt", hidden, down_first, preferred_element_type=jnp.float32
    ).astype(jnp.bfloat16)
    return mixed, hidden, lowered


def backward_middle(mixed, grad_lowered_r, up_second, down_first):
    grad_hidden = jnp.einsum(
        "prt,rop->rot", grad_lowered_r, down_first, preferred_element_type=jnp.float32
    )
    sigmoid_gate = jax.nn.sigmoid(mixed[0])
    slope = sigmoid_gate * (1.0 + mixed[0] * (1.0 - sigmoid_gate))
    grad_mixed = jnp.stack(
        [grad_hidden * mixed[1] * slope, grad_hidden * mixed[0] * sigmoid_gate]
    ).astype(jnp.bfloat16)
    grad_spread = jnp.einsum(
        "grot,grpo->grpt", grad_mixed, up_second, preferred_element_type=jnp.float32
    ).astype(jnp.bfloat16)
    return grad_mixed, grad_spread


def output_of(values, lowered_p, down_second):
    added = jnp.einsum("rpt,prq->pqt", lowered_p, down_second, preferred_element_type=jnp.float32)
    return (values.astype(jnp.float32) + added).astype(jnp.bfloat16)


def input_grad_of(grads, grad_spread_p, up_first):
    added = jnp.einsum(
        "rpgt,gpqr->pqt", grad_spread_p, up_first, preferred_element_type=jnp.float32
    )
    return (grads.astype(jnp.float32) + added).astype(jnp.bfloat16)


def shards(
    held_input,
    fresh_input,
    stashed,
    held_grad,
    fresh_grad,
    first_up,
    second_up,
    first_down,
    second_down,
):
    feature_blocks = first_up.shape[2]
    hidden_blocks = second_up.shape[2]
    tokens = held_input.shape[2]
    up_first = first_up[0].reshape(2, feature_blocks, FIRST_IN, SECOND_BLOCKS)
    up_second = second_up[0].reshape(2, hidden_blocks, FIRST_BLOCKS, BLOCK)
    down_first = first_down[0].reshape(hidden_blocks, BLOCK, FIRST_BLOCKS)
    down_second = second_down[0].reshape(feature_blocks, SECOND_BLOCKS, FIRST_IN)
    first_inputs = held_input[0].reshape(feature_blocks, FIRST_IN, tokens)
    first_grads = held_grad[0].reshape(feature_blocks, FIRST_IN, tokens)
    stash_views = [
        stashed[0, k].reshape(feature_blocks, FIRST_IN, tokens) for k in range(TICKS)
    ]
    section_pos = lax.axis_index("section")
    last_section = lax.axis_size("section") - 1
    t = tokens

    values_a = jnp.concatenate([first_inputs] + stash_views, axis=2)
    spread_a = spread_of(values_a, up_first)
    glow_1 = lowered_grad_of(first_grads, down_second)
    payload = jnp.concatenate(
        [spread_a.reshape(feature_blocks, SECOND_BLOCKS, 2 * 3 * t), glow_1], axis=2
    )
    arrived = to_blocks(payload)
    spread_ar = arrived[:, :, : 6 * t].reshape(FIRST_BLOCKS, hidden_blocks, 2, 3 * t)
    glow_1r = arrived[:, :, 6 * t :]
    mixed_a, hidden_a, lowered_a = forward_middle(spread_ar, up_second, down_first)
    gmix_1, gspread_1 = backward_middle(mixed_a[:, :, :, t : 2 * t], glow_1r, up_second, down_first)
    payload = jnp.concatenate([lowered_a, gspread_1[0], gspread_1[1]], axis=2)
    back = to_features(payload)
    lowered_ap = back[:, :, : 3 * t]
    gspread_1p = back[:, :, 3 * t :].reshape(SECOND_BLOCKS, feature_blocks, 2, t)
    outputs = output_of(first_inputs, lowered_ap[:, :, :t], down_second)
    backward = input_grad_of(first_grads, gspread_1p, up_first)

    moved_forward = from_behind(outputs, "section", 1)
    inputs = jnp.where(
        section_pos == 0,
        fresh_input.reshape(feature_blocks, FIRST_IN, tokens),
        moved_forward,
    )
    moved_backward = from_behind(backward, "section", -1)
    grads = jnp.where(
        section_pos == last_section,
        fresh_grad.reshape(feature_blocks, FIRST_IN, tokens),
        moved_backward,
    )

    spread_b = spread_of(inputs, up_first)
    glow_2 = lowered_grad_of(grads, down_second)
    payload = jnp.concatenate(
        [spread_b.reshape(feature_blocks, SECOND_BLOCKS, 2 * t), glow_2], axis=2
    )
    arrived = to_blocks(payload)
    spread_br = arrived[:, :, : 2 * t].reshape(FIRST_BLOCKS, hidden_blocks, 2, t)
    glow_2r = arrived[:, :, 2 * t :]
    _, _, lowered_b = forward_middle(spread_br, up_second, down_first)
    gmix_2, gspread_2 = backward_middle(
        mixed_a[:, :, :, 2 * t :], glow_2r, up_second, down_first
    )
    payload = jnp.concatenate([lowered_b, gspread_2[0], gspread_2[1]], axis=2)
    back = to_features(payload)
    lowered_bp = back[:, :, :t]
    gspread_2p = back[:, :, t:].reshape(SECOND_BLOCKS, feature_blocks, 2, t)
    outputs = output_of(inputs, lowered_bp, down_second)
    backward = input_grad_of(grads, gspread_2p, up_first)

    stash_both = jnp.concatenate(stash_views, axis=2)
    gspread_both = jnp.concatenate([gspread_1p, gspread_2p], axis=3)
    spread_both = spread_ar[:, :, :, t:]
    gmix_both = jnp.concatenate([gmix_1, gmix_2], axis=3)
    hidden_both = hidden_a[:, :, t:]
    glow_both = jnp.concatenate([glow_1r, glow_2r], axis=2)
    lowered_both = lowered_ap[:, :, t:]
    grads_both = jnp.concatenate([first_grads, grads], axis=2)
    total_first_up = jnp.einsum(
        "pqt,rpgt->gpqr", stash_both, gspread_both, preferred_element_type=jnp.float32
    )
    total_second_up = jnp.einsum(
        "prgt,grot->grpo", spread_both, gmix_both, preferred_element_type=jnp.float32
    )
    total_first_down = jnp.einsum(
        "rot,prt->rop", hidden_both, glow_both, preferred_element_type=jnp.float32
    )
    total_second_down = jnp.einsum(
        "rpt,pqt->prq", lowered_both, grads_both, preferred_element_type=jnp.float32
    )
    factor = 1.0 / math.sqrt(TICKS * tokens)
    return (
        outputs.reshape(held_input.shape),
        backward.reshape(held_grad.shape),
        (total_first_up * factor).astype(jnp.bfloat16).reshape(first_up.shape),
        (total_second_up * factor).astype(jnp.bfloat16).reshape(second_up.shape),
        (total_first_down * factor).astype(jnp.bfloat16).reshape(first_down.shape),
        (total_second_down * factor).astype(jnp.bfloat16).reshape(second_down.shape),
    )


def solution(mesh):
    return jax.shard_map(
        shards,
        mesh=mesh,
        in_specs=(
            P("section", "blk", None),
            P("blk", None),
            P("section", None, "blk", None),
            P("section", "blk", None),
            P("blk", None),
            P("section", None, "blk", None),
            P("section", None, "blk", None),
            P("section", "blk", None),
            P("section", "blk", None),
        ),
        out_specs=(
            P("section", "blk", None),
            P("section", "blk", None),
            P("section", None, "blk", None),
            P("section", None, "blk", None),
            P("section", "blk", None),
            P("section", "blk", None),
        ),
        check_vma=False,
    )
```

```python
import functools
import math

import jax
import jax.numpy as jnp
from jax import lax
from jax.experimental import pallas as pl
from jax.experimental.pallas import tpu as pltpu
from jax.sharding import PartitionSpec as P

BLOCK = 128
FIRST_BLOCKS = 128
FIRST_IN = 40
SECOND_BLOCKS = 160
TICKS = 2


def from_behind(value, axis, by):
    length = lax.axis_size(axis)
    pairs = [(i, i + by) for i in range(length) if 0 <= i + by < length]
    return lax.ppermute(value, axis, pairs)


def to_blocks(pieces):
    return lax.all_to_all(pieces, "blk", split_axis=1, concat_axis=0, tiled=True)


def to_features(pieces):
    groups = lax.axis_size("blk")
    r_local, p_all, n = pieces.shape
    p_local = p_all // groups
    grouped = pieces.reshape(r_local, groups, p_local, n).transpose(1, 0, 2, 3)
    arrived = lax.all_to_all(grouped, "blk", split_axis=0, concat_axis=0, tiled=True)
    return arrived.reshape(groups * r_local, p_local, n)


def spread_of(values, up_first):
    return jnp.einsum(
        "pqt,gpqr->prgt", values, up_first, preferred_element_type=jnp.float32
    ).astype(jnp.bfloat16)


def lowered_grad_of(grads, down_second):
    return jnp.einsum(
        "pqt,prq->prt", grads, down_second, preferred_element_type=jnp.float32
    ).astype(jnp.bfloat16)


def _middle_kernel(fwd, bwd, bwd_at, keep_at, has_mixed_in, *refs):
    refs = list(refs)
    arrived, up, up_t, down, down_t = refs[:5]
    refs = refs[5:]
    mixed_in = refs.pop(0) if has_mixed_in else None
    payload, grad_mixed = refs[0], refs[1]
    rest = refs[2:]
    hidden_out = rest.pop(0) if not has_mixed_in else None
    keep_out = rest.pop(0) if keep_at is not None else None
    for r in range(arrived.shape[0]):
        gate = jnp.dot(up_t[0, r], arrived[r, :, :fwd], preferred_element_type=jnp.float32)
        upper = jnp.dot(
            up_t[1, r], arrived[r, :, fwd : 2 * fwd], preferred_element_type=jnp.float32
        )
        hidden = (gate / (1.0 + jnp.exp(-gate)) * upper).astype(jnp.bfloat16)
        payload[r, :, :fwd] = jnp.dot(
            down_t[r], hidden, preferred_element_type=jnp.float32
        ).astype(jnp.bfloat16)
        if hidden_out is not None:
            hidden_out[r] = hidden
        if keep_out is not None:
            keep_out[0, r] = gate[:, keep_at : keep_at + bwd]
            keep_out[1, r] = upper[:, keep_at : keep_at + bwd]
        if has_mixed_in:
            m0, m1 = mixed_in[0, r], mixed_in[1, r]
        else:
            m0, m1 = gate[:, bwd_at : bwd_at + bwd], upper[:, bwd_at : bwd_at + bwd]
        grad_hidden = jnp.dot(
            down[r], arrived[r, :, 2 * fwd :], preferred_element_type=jnp.float32
        )
        sg = 1.0 / (1.0 + jnp.exp(-m0))
        gm0 = (grad_hidden * m1 * (sg * (1.0 + m0 * (1.0 - sg)))).astype(jnp.bfloat16)
        gm1 = (grad_hidden * m0 * sg).astype(jnp.bfloat16)
        grad_mixed[0, r] = gm0
        grad_mixed[1, r] = gm1
        payload[r, :, fwd : fwd + bwd] = jnp.dot(
            up[0, r], gm0, preferred_element_type=jnp.float32
        ).astype(jnp.bfloat16)
        payload[r, :, fwd + bwd :] = jnp.dot(
            up[1, r], gm1, preferred_element_type=jnp.float32
        ).astype(jnp.bfloat16)


def middle(arrived, up, up_t, down, down_t, fwd, bwd, bwd_at=0, keep_at=None, mixed_in=None):
    rb, pa, _ = arrived.shape
    o = up.shape[3]
    outs = [
        jax.ShapeDtypeStruct((rb, pa, fwd + 2 * bwd), jnp.bfloat16),
        jax.ShapeDtypeStruct((2, rb, o, bwd), jnp.bfloat16),
    ]
    if mixed_in is None:
        outs.append(jax.ShapeDtypeStruct((rb, o, fwd), jnp.bfloat16))
    if keep_at is not None:
        outs.append(jax.ShapeDtypeStruct((2, rb, o, bwd), jnp.float32))
    ins = [arrived, up, up_t, down, down_t] + ([mixed_in] if mixed_in is not None else [])
    flops = 2 * rb * o * pa * (3 * fwd + 3 * bwd)
    bytes_accessed = sum(x.size * x.dtype.itemsize for x in ins) + sum(
        math.prod(s.shape) * s.dtype.itemsize for s in outs
    )
    vmem = pltpu.MemorySpace.VMEM
    return pl.pallas_call(
        functools.partial(_middle_kernel, fwd, bwd, bwd_at, keep_at, mixed_in is not None),
        out_shape=tuple(outs),
        in_specs=[pl.BlockSpec(memory_space=vmem)] * len(ins),
        out_specs=tuple(pl.BlockSpec(memory_space=vmem) for _ in outs),
        cost_estimate=pl.CostEstimate(
            flops=flops, transcendentals=rb * o * (fwd + bwd), bytes_accessed=bytes_accessed
        ),
    )(*ins)


def output_of(values, lowered_p, down_second):
    added = jnp.einsum("rpt,prq->pqt", lowered_p, down_second, preferred_element_type=jnp.float32)
    return (values.astype(jnp.float32) + added).astype(jnp.bfloat16)


def input_grad_of(grads, grad_spread_p, up_first):
    added = jnp.einsum(
        "rpgt,gpqr->pqt", grad_spread_p, up_first, preferred_element_type=jnp.float32
    )
    return (grads.astype(jnp.float32) + added).astype(jnp.bfloat16)


def shards(
    held_input,
    fresh_input,
    stashed,
    held_grad,
    fresh_grad,
    first_up,
    second_up,
    first_down,
    second_down,
):
    pb = first_up.shape[2]
    rb = second_up.shape[2]
    t = held_input.shape[2]
    up_first = first_up[0].reshape(2, pb, FIRST_IN, SECOND_BLOCKS)
    up_second = second_up[0].reshape(2, rb, FIRST_BLOCKS, BLOCK)
    down_first = first_down[0].reshape(rb, BLOCK, FIRST_BLOCKS)
    down_second = second_down[0].reshape(pb, SECOND_BLOCKS, FIRST_IN)
    up_second_t = jnp.swapaxes(up_second, 2, 3)
    down_first_t = jnp.swapaxes(down_first, 1, 2)
    first_inputs = held_input[0].reshape(pb, FIRST_IN, t)
    first_grads = held_grad[0].reshape(pb, FIRST_IN, t)
    stash_0 = stashed[0, 0].reshape(pb, FIRST_IN, t)
    stash_1 = stashed[0, 1].reshape(pb, FIRST_IN, t)
    section_pos = lax.axis_index("section")
    last_section = lax.axis_size("section") - 1
    weights = (up_second, up_second_t, down_first, down_first_t)

    spread_a = spread_of(jnp.concatenate([first_inputs, stash_0, stash_1], axis=2), up_first)
    glow_1 = lowered_grad_of(first_grads, down_second)
    payload = jnp.concatenate([spread_a.reshape(pb, SECOND_BLOCKS, 6 * t), glow_1], axis=2)
    arrived_a = jnp.swapaxes(to_blocks(payload), 0, 1)
    payload_a, gmix_1, hidden_a, mixed_s1 = middle(
        arrived_a, *weights, fwd=3 * t, bwd=t, bwd_at=t, keep_at=2 * t
    )
    back = to_features(payload_a)
    lowered_ap = back[:, :, : 3 * t]
    gspread_1p = back[:, :, 3 * t :].reshape(SECOND_BLOCKS, pb, 2, t)
    outputs = output_of(first_inputs, lowered_ap[:, :, :t], down_second)
    backward = input_grad_of(first_grads, gspread_1p, up_first)

    moved_forward = from_behind(outputs, "section", 1)
    inputs = jnp.where(section_pos == 0, fresh_input.reshape(pb, FIRST_IN, t), moved_forward)
    moved_backward = from_behind(backward, "section", -1)
    grads = jnp.where(
        section_pos == last_section, fresh_grad.reshape(pb, FIRST_IN, t), moved_backward
    )

    spread_b = spread_of(inputs, up_first)
    glow_2 = lowered_grad_of(grads, down_second)
    payload = jnp.concatenate([spread_b.reshape(pb, SECOND_BLOCKS, 2 * t), glow_2], axis=2)
    arrived_b = jnp.swapaxes(to_blocks(payload), 0, 1)
    payload_b, gmix_2 = middle(arrived_b, *weights, fwd=t, bwd=t, mixed_in=mixed_s1)
    back = to_features(payload_b)
    outputs = output_of(inputs, back[:, :, :t], down_second)
    gspread_2p = back[:, :, t:].reshape(SECOND_BLOCKS, pb, 2, t)
    backward = input_grad_of(grads, gspread_2p, up_first)

    stash_both = jnp.concatenate([stash_0, stash_1], axis=2)
    gspread_both = jnp.concatenate([gspread_1p, gspread_2p], axis=3)
    spread_both = jnp.stack(
        [arrived_a[:, :, t : 3 * t], arrived_a[:, :, 4 * t : 6 * t]]
    )
    gmix_both = jnp.concatenate([gmix_1, gmix_2], axis=3)
    hidden_both = hidden_a[:, :, t:]
    glow_both = jnp.concatenate([arrived_a[:, :, 6 * t :], arrived_b[:, :, 2 * t :]], axis=2)
    lowered_both = lowered_ap[:, :, t:]
    grads_both = jnp.concatenate([first_grads, grads], axis=2)
    total_first_up = jnp.einsum(
        "pqt,rpgt->gpqr", stash_both, gspread_both, preferred_element_type=jnp.float32
    )
    total_second_up = jnp.einsum(
        "grpt,grot->grpo", spread_both, gmix_both, preferred_element_type=jnp.float32
    )
    total_first_down = jnp.einsum(
        "rot,rpt->rop", hidden_both, glow_both, preferred_element_type=jnp.float32
    )
    total_second_down = jnp.einsum(
        "rpt,pqt->prq", lowered_both, grads_both, preferred_element_type=jnp.float32
    )
    factor = 1.0 / math.sqrt(TICKS * t)
    return (
        outputs.reshape(held_input.shape),
        backward.reshape(held_grad.shape),
        (total_first_up * factor).astype(jnp.bfloat16).reshape(first_up.shape),
        (total_second_up * factor).astype(jnp.bfloat16).reshape(second_up.shape),
        (total_first_down * factor).astype(jnp.bfloat16).reshape(first_down.shape),
        (total_second_down * factor).astype(jnp.bfloat16).reshape(second_down.shape),
    )


def solution(mesh):
    return jax.shard_map(
        shards,
        mesh=mesh,
        in_specs=(
            P("section", "blk", None),
            P("blk", None),
            P("section", None, "blk", None),
            P("section", "blk", None),
            P("blk", None),
            P("section", None, "blk", None),
            P("section", None, "blk", None),
            P("section", "blk", None),
            P("section", "blk", None),
        ),
        out_specs=(
            P("section", "blk", None),
            P("section", "blk", None),
            P("section", None, "blk", None),
            P("section", None, "blk", None),
            P("section", "blk", None),
            P("section", "blk", None),
        ),
        check_vma=False,
    )
```

```python
import functools
import math

import jax
import jax.numpy as jnp
from jax import lax
from jax.experimental import pallas as pl
from jax.experimental.pallas import tpu as pltpu
from jax.sharding import PartitionSpec as P

BLOCK = 128
FIRST_BLOCKS = 128
FIRST_IN = 40
SECOND_BLOCKS = 160
TICKS = 2


def from_behind(value, axis, by):
    length = lax.axis_size(axis)
    pairs = [(i, i + by) for i in range(length) if 0 <= i + by < length]
    return lax.ppermute(value, axis, pairs)


def to_blocks(pieces):
    return lax.all_to_all(pieces, "blk", split_axis=1, concat_axis=0, tiled=True)


def to_features(pieces):
    groups = lax.axis_size("blk")
    r_local, p_all, n = pieces.shape
    p_local = p_all // groups
    grouped = pieces.reshape(r_local, groups, p_local, n).transpose(1, 0, 2, 3)
    arrived = lax.all_to_all(grouped, "blk", split_axis=0, concat_axis=0, tiled=True)
    return arrived.reshape(groups * r_local, p_local, n)


def spread_of(values, up_first):
    return jnp.einsum(
        "pqt,gpqr->prgt", values, up_first, preferred_element_type=jnp.float32
    ).astype(jnp.bfloat16)


def lowered_grad_of(grads, down_second):
    return jnp.einsum(
        "pqt,prq->prt", grads, down_second, preferred_element_type=jnp.float32
    ).astype(jnp.bfloat16)


def _middle_kernel(fwd, bwd, bwd_at, keep_hidden, recompute, *refs):
    refs = list(refs)
    arrived, up, up_t, down, down_t = refs[:5]
    refs = refs[5:]
    if recompute:
        gate_src, up_src = refs[0], refs[1]
        refs = refs[2:]
    payload, grad_mixed = refs[0], refs[1]
    hidden_out = refs[2] if keep_hidden else None
    gate = jnp.dot(up_t[0, 0], arrived[0, :, :fwd], preferred_element_type=jnp.float32)
    upper = jnp.dot(
        up_t[1, 0], arrived[0, :, fwd : 2 * fwd], preferred_element_type=jnp.float32
    )
    hidden = (gate / (1.0 + jnp.exp(-gate)) * upper).astype(jnp.bfloat16)
    payload[0, :, :fwd] = jnp.dot(
        down_t[0], hidden, preferred_element_type=jnp.float32
    ).astype(jnp.bfloat16)
    if hidden_out is not None:
        hidden_out[0] = hidden[:, bwd_at:]
    if recompute:
        m0 = jnp.dot(up_t[0, 0], gate_src[0], preferred_element_type=jnp.float32)
        m1 = jnp.dot(up_t[1, 0], up_src[0], preferred_element_type=jnp.float32)
    else:
        m0, m1 = gate[:, bwd_at : bwd_at + bwd], upper[:, bwd_at : bwd_at + bwd]
    grad_hidden = jnp.dot(down[0], arrived[0, :, 2 * fwd :], preferred_element_type=jnp.float32)
    sg = 1.0 / (1.0 + jnp.exp(-m0))
    gm0 = (grad_hidden * m1 * (sg * (1.0 + m0 * (1.0 - sg)))).astype(jnp.bfloat16)
    gm1 = (grad_hidden * m0 * sg).astype(jnp.bfloat16)
    grad_mixed[0, 0] = gm0
    grad_mixed[1, 0] = gm1
    payload[0, :, fwd : fwd + bwd] = jnp.dot(
        up[0, 0], gm0, preferred_element_type=jnp.float32
    ).astype(jnp.bfloat16)
    payload[0, :, fwd + bwd :] = jnp.dot(
        up[1, 0], gm1, preferred_element_type=jnp.float32
    ).astype(jnp.bfloat16)


def middle(arrived, up, up_t, down, down_t, fwd, bwd, bwd_at=0, keep_hidden=False, source=None):
    rb, pa, _ = arrived.shape
    o = up.shape[3]
    outs = [
        jax.ShapeDtypeStruct((rb, pa, fwd + 2 * bwd), jnp.bfloat16),
        jax.ShapeDtypeStruct((2, rb, o, bwd), jnp.bfloat16),
    ]
    out_specs = [
        pl.BlockSpec((1, pa, fwd + 2 * bwd), lambda r: (r, 0, 0)),
        pl.BlockSpec((2, 1, o, bwd), lambda r: (0, r, 0, 0)),
    ]
    if keep_hidden:
        outs.append(jax.ShapeDtypeStruct((rb, o, fwd - bwd_at), jnp.bfloat16))
        out_specs.append(pl.BlockSpec((1, o, fwd - bwd_at), lambda r: (r, 0, 0)))
    ins = [arrived, up, up_t, down, down_t]
    in_specs = [
        pl.BlockSpec((1, pa, arrived.shape[2]), lambda r: (r, 0, 0)),
        pl.BlockSpec((2, 1) + up.shape[2:], lambda r: (0, r, 0, 0)),
        pl.BlockSpec((2, 1) + up_t.shape[2:], lambda r: (0, r, 0, 0)),
        pl.BlockSpec((1,) + down.shape[1:], lambda r: (r, 0, 0)),
        pl.BlockSpec((1,) + down_t.shape[1:], lambda r: (r, 0, 0)),
    ]
    if source is not None:
        held, gate_block, up_block = source
        ins += [held, held]
        in_specs += [
            pl.BlockSpec((1, pa, bwd), lambda r, b=gate_block: (r, 0, b)),
            pl.BlockSpec((1, pa, bwd), lambda r, b=up_block: (r, 0, b)),
        ]
    flops = 2 * rb * o * pa * (3 * fwd + (5 if source is not None else 3) * bwd)
    bytes_accessed = sum(x.size * x.dtype.itemsize for x in ins[:5]) + sum(
        math.prod(s.shape) * s.dtype.itemsize for s in outs
    )
    return pl.pallas_call(
        functools.partial(
            _middle_kernel, fwd, bwd, bwd_at, keep_hidden, source is not None
        ),
        out_shape=tuple(outs),
        grid=(rb,),
        in_specs=in_specs,
        out_specs=tuple(out_specs),
        cost_estimate=pl.CostEstimate(
            flops=flops, transcendentals=rb * o * (fwd + bwd), bytes_accessed=bytes_accessed
        ),
    )(*ins)


def output_of(values, lowered_p, down_second):
    added = jnp.einsum("rpt,prq->pqt", lowered_p, down_second, preferred_element_type=jnp.float32)
    return (values.astype(jnp.float32) + added).astype(jnp.bfloat16)


def input_grad_of(grads, grad_spread_p, up_first):
    added = jnp.einsum(
        "rpgt,gpqr->pqt", grad_spread_p, up_first, preferred_element_type=jnp.float32
    )
    return (grads.astype(jnp.float32) + added).astype(jnp.bfloat16)


def shards(
    held_input,
    fresh_input,
    stashed,
    held_grad,
    fresh_grad,
    first_up,
    second_up,
    first_down,
    second_down,
):
    pb = first_up.shape[2]
    rb = second_up.shape[2]
    t = held_input.shape[2]
    up_first = first_up[0].reshape(2, pb, FIRST_IN, SECOND_BLOCKS)
    up_second = second_up[0].reshape(2, rb, FIRST_BLOCKS, BLOCK)
    down_first = first_down[0].reshape(rb, BLOCK, FIRST_BLOCKS)
    down_second = second_down[0].reshape(pb, SECOND_BLOCKS, FIRST_IN)
    up_second_t = jnp.swapaxes(up_second, 2, 3)
    down_first_t = jnp.swapaxes(down_first, 1, 2)
    first_inputs = held_input[0].reshape(pb, FIRST_IN, t)
    first_grads = held_grad[0].reshape(pb, FIRST_IN, t)
    stash_0 = stashed[0, 0].reshape(pb, FIRST_IN, t)
    stash_1 = stashed[0, 1].reshape(pb, FIRST_IN, t)
    section_pos = lax.axis_index("section")
    last_section = lax.axis_size("section") - 1
    weights = (up_second, up_second_t, down_first, down_first_t)

    spread_a = spread_of(jnp.concatenate([first_inputs, stash_0, stash_1], axis=2), up_first)
    glow_1 = lowered_grad_of(first_grads, down_second)
    payload = jnp.concatenate([spread_a.reshape(pb, SECOND_BLOCKS, 6 * t), glow_1], axis=2)
    arrived_a = jnp.swapaxes(to_blocks(payload), 0, 1)
    payload_a, gmix_1, hidden_both = middle(
        arrived_a, *weights, fwd=3 * t, bwd=t, bwd_at=t, keep_hidden=True
    )
    back = to_features(payload_a)
    lowered_ap = back[:, :, : 3 * t]
    gspread_1p = back[:, :, 3 * t :].reshape(SECOND_BLOCKS, pb, 2, t)
    outputs = output_of(first_inputs, lowered_ap[:, :, :t], down_second)
    backward = input_grad_of(first_grads, gspread_1p, up_first)

    moved_forward = from_behind(outputs, "section", 1)
    inputs = jnp.where(section_pos == 0, fresh_input.reshape(pb, FIRST_IN, t), moved_forward)
    moved_backward = from_behind(backward, "section", -1)
    grads = jnp.where(
        section_pos == last_section, fresh_grad.reshape(pb, FIRST_IN, t), moved_backward
    )

    spread_b = spread_of(inputs, up_first)
    glow_2 = lowered_grad_of(grads, down_second)
    payload = jnp.concatenate([spread_b.reshape(pb, SECOND_BLOCKS, 2 * t), glow_2], axis=2)
    arrived_b = jnp.swapaxes(to_blocks(payload), 0, 1)
    payload_b, gmix_2 = middle(arrived_b, *weights, fwd=t, bwd=t, source=(arrived_a, 2, 5))
    back = to_features(payload_b)
    outputs = output_of(inputs, back[:, :, :t], down_second)
    gspread_2p = back[:, :, t:].reshape(SECOND_BLOCKS, pb, 2, t)
    backward = input_grad_of(grads, gspread_2p, up_first)

    stash_both = jnp.concatenate([stash_0, stash_1], axis=2)
    gspread_both = jnp.concatenate([gspread_1p, gspread_2p], axis=3)
    spread_both = jnp.stack(
        [arrived_a[:, :, t : 3 * t], arrived_a[:, :, 4 * t : 6 * t]]
    )
    gmix_both = jnp.concatenate([gmix_1, gmix_2], axis=3)
    glow_both = jnp.concatenate([arrived_a[:, :, 6 * t :], arrived_b[:, :, 2 * t :]], axis=2)
    lowered_both = lowered_ap[:, :, t:]
    grads_both = jnp.concatenate([first_grads, grads], axis=2)
    total_first_up = jnp.einsum(
        "pqt,rpgt->gpqr", stash_both, gspread_both, preferred_element_type=jnp.float32
    )
    total_second_up = jnp.einsum(
        "grpt,grot->grpo", spread_both, gmix_both, preferred_element_type=jnp.float32
    )
    total_first_down = jnp.einsum(
        "rot,rpt->rop", hidden_both, glow_both, preferred_element_type=jnp.float32
    )
    total_second_down = jnp.einsum(
        "rpt,pqt->prq", lowered_both, grads_both, preferred_element_type=jnp.float32
    )
    factor = 1.0 / math.sqrt(TICKS * t)
    return (
        outputs.reshape(held_input.shape),
        backward.reshape(held_grad.shape),
        (total_first_up * factor).astype(jnp.bfloat16).reshape(first_up.shape),
        (total_second_up * factor).astype(jnp.bfloat16).reshape(second_up.shape),
        (total_first_down * factor).astype(jnp.bfloat16).reshape(first_down.shape),
        (total_second_down * factor).astype(jnp.bfloat16).reshape(second_down.shape),
    )


def solution(mesh):
    return jax.shard_map(
        shards,
        mesh=mesh,
        in_specs=(
            P("section", "blk", None),
            P("blk", None),
            P("section", None, "blk", None),
            P("section", "blk", None),
            P("blk", None),
            P("section", None, "blk", None),
            P("section", None, "blk", None),
            P("section", "blk", None),
            P("section", "blk", None),
        ),
        out_specs=(
            P("section", "blk", None),
            P("section", "blk", None),
            P("section", None, "blk", None),
            P("section", None, "blk", None),
            P("section", "blk", None),
            P("section", "blk", None),
        ),
        check_vma=False,
    )
```

```python
import functools
import math

import jax
import jax.numpy as jnp
from jax import lax
from jax.experimental import pallas as pl
from jax.experimental.pallas import tpu as pltpu
from jax.sharding import PartitionSpec as P

BLOCK = 128
FIRST_BLOCKS = 128
FIRST_IN = 40
SECOND_BLOCKS = 160
TICKS = 2


def from_behind(value, axis, by):
    length = lax.axis_size(axis)
    pairs = [(i, i + by) for i in range(length) if 0 <= i + by < length]
    return lax.ppermute(value, axis, pairs)


def to_blocks(pieces):
    return lax.all_to_all(pieces, "blk", split_axis=1, concat_axis=0, tiled=True)


def to_features(grouped):
    groups, r_local, p_local, n = grouped.shape
    arrived = lax.all_to_all(grouped, "blk", split_axis=0, concat_axis=0, tiled=True)
    return arrived.reshape(groups * r_local, p_local, n)


def spread_of(values, up_first):
    return jnp.einsum(
        "pqt,gpqr->prgt", values, up_first, preferred_element_type=jnp.float32
    ).astype(jnp.bfloat16)


def lowered_grad_of(grads, down_second):
    return jnp.einsum(
        "pqt,prq->prt", grads, down_second, preferred_element_type=jnp.float32
    ).astype(jnp.bfloat16)


def put(payload, r, at, value):
    rows = payload.shape[2]
    width = value.shape[1]
    for group in range(payload.shape[0]):
        payload[group, r, :, at : at + width] = value[group * rows : (group + 1) * rows].astype(
            payload.dtype
        )


def _middle_kernel(fwd, bwd, bwd_at, keep_at, has_mixed_in, *refs):
    refs = list(refs)
    arrived, up, up_t, down, down_t = refs[:5]
    refs = refs[5:]
    mixed_in = refs.pop(0) if has_mixed_in else None
    payload, grad_mixed = refs[0], refs[1]
    rest = refs[2:]
    hidden_out = rest.pop(0) if not has_mixed_in else None
    keep_out = rest.pop(0) if keep_at is not None else None
    for r in range(arrived.shape[0]):
        gate = jnp.dot(up_t[0, r], arrived[r, :, :fwd], preferred_element_type=jnp.float32)
        upper = jnp.dot(
            up_t[1, r], arrived[r, :, fwd : 2 * fwd], preferred_element_type=jnp.float32
        )
        hidden = (gate / (1.0 + jnp.exp(-gate)) * upper).astype(jnp.bfloat16)
        put(payload, r, 0, jnp.dot(down_t[r], hidden, preferred_element_type=jnp.float32))
        if hidden_out is not None:
            hidden_out[r] = hidden
        if keep_out is not None:
            keep_out[0, r] = gate[:, keep_at : keep_at + bwd]
            keep_out[1, r] = upper[:, keep_at : keep_at + bwd]
        if has_mixed_in:
            m0, m1 = mixed_in[0, r], mixed_in[1, r]
        else:
            m0, m1 = gate[:, bwd_at : bwd_at + bwd], upper[:, bwd_at : bwd_at + bwd]
        grad_hidden = jnp.dot(
            down[r], arrived[r, :, 2 * fwd :], preferred_element_type=jnp.float32
        )
        sg = 1.0 / (1.0 + jnp.exp(-m0))
        gm0 = (grad_hidden * m1 * (sg * (1.0 + m0 * (1.0 - sg)))).astype(jnp.bfloat16)
        gm1 = (grad_hidden * m0 * sg).astype(jnp.bfloat16)
        grad_mixed[0, r] = gm0
        grad_mixed[1, r] = gm1
        put(payload, r, fwd, jnp.dot(up[0, r], gm0, preferred_element_type=jnp.float32))
        put(payload, r, fwd + bwd, jnp.dot(up[1, r], gm1, preferred_element_type=jnp.float32))


def middle(arrived, up, up_t, down, down_t, fwd, bwd, bwd_at=0, keep_at=None, mixed_in=None):
    rb, pa, _ = arrived.shape
    o = up.shape[3]
    groups = lax.axis_size("blk")
    outs = [
        jax.ShapeDtypeStruct((groups, rb, pa // groups, fwd + 2 * bwd), jnp.bfloat16),
        jax.ShapeDtypeStruct((2, rb, o, bwd), jnp.bfloat16),
    ]
    if mixed_in is None:
        outs.append(jax.ShapeDtypeStruct((rb, o, fwd), jnp.bfloat16))
    if keep_at is not None:
        outs.append(jax.ShapeDtypeStruct((2, rb, o, bwd), jnp.float32))
    ins = [arrived, up, up_t, down, down_t] + ([mixed_in] if mixed_in is not None else [])
    flops = 2 * rb * o * pa * (3 * fwd + 3 * bwd)
    bytes_accessed = sum(x.size * x.dtype.itemsize for x in ins) + sum(
        math.prod(s.shape) * s.dtype.itemsize for s in outs
    )
    vmem = pltpu.MemorySpace.VMEM
    return pl.pallas_call(
        functools.partial(_middle_kernel, fwd, bwd, bwd_at, keep_at, mixed_in is not None),
        out_shape=tuple(outs),
        in_specs=[pl.BlockSpec(memory_space=vmem)] * len(ins),
        out_specs=tuple(pl.BlockSpec(memory_space=vmem) for _ in outs),
        cost_estimate=pl.CostEstimate(
            flops=flops, transcendentals=rb * o * (fwd + bwd), bytes_accessed=bytes_accessed
        ),
    )(*ins)


def output_of(values, lowered_p, down_second):
    added = jnp.einsum("rpt,prq->pqt", lowered_p, down_second, preferred_element_type=jnp.float32)
    return (values.astype(jnp.float32) + added).astype(jnp.bfloat16)


def input_grad_of(grads, grad_spread_p, up_first):
    added = jnp.einsum(
        "rpgt,gpqr->pqt", grad_spread_p, up_first, preferred_element_type=jnp.float32
    )
    return (grads.astype(jnp.float32) + added).astype(jnp.bfloat16)


def shards(
    held_input,
    fresh_input,
    stashed,
    held_grad,
    fresh_grad,
    first_up,
    second_up,
    first_down,
    second_down,
):
    pb = first_up.shape[2]
    rb = second_up.shape[2]
    t = held_input.shape[2]
    up_first = first_up[0].reshape(2, pb, FIRST_IN, SECOND_BLOCKS)
    up_second = second_up[0].reshape(2, rb, FIRST_BLOCKS, BLOCK)
    down_first = first_down[0].reshape(rb, BLOCK, FIRST_BLOCKS)
    down_second = second_down[0].reshape(pb, SECOND_BLOCKS, FIRST_IN)
    up_second_t = jnp.swapaxes(up_second, 2, 3)
    down_first_t = jnp.swapaxes(down_first, 1, 2)
    first_inputs = held_input[0].reshape(pb, FIRST_IN, t)
    first_grads = held_grad[0].reshape(pb, FIRST_IN, t)
    stash_0 = stashed[0, 0].reshape(pb, FIRST_IN, t)
    stash_1 = stashed[0, 1].reshape(pb, FIRST_IN, t)
    section_pos = lax.axis_index("section")
    last_section = lax.axis_size("section") - 1
    weights = (up_second, up_second_t, down_first, down_first_t)

    spread_a = spread_of(jnp.concatenate([first_inputs, stash_0, stash_1], axis=2), up_first)
    glow_1 = lowered_grad_of(first_grads, down_second)
    payload = jnp.concatenate([spread_a.reshape(pb, SECOND_BLOCKS, 6 * t), glow_1], axis=2)
    arrived_a = jnp.swapaxes(to_blocks(payload), 0, 1)
    payload_a, gmix_1, hidden_a, mixed_s1 = middle(
        arrived_a, *weights, fwd=3 * t, bwd=t, bwd_at=t, keep_at=2 * t
    )
    back = to_features(payload_a)
    lowered_ap = back[:, :, : 3 * t]
    gspread_1p = back[:, :, 3 * t :].reshape(SECOND_BLOCKS, pb, 2, t)
    outputs = output_of(first_inputs, lowered_ap[:, :, :t], down_second)
    backward = input_grad_of(first_grads, gspread_1p, up_first)

    moved_forward = from_behind(outputs, "section", 1)
    inputs = jnp.where(section_pos == 0, fresh_input.reshape(pb, FIRST_IN, t), moved_forward)
    moved_backward = from_behind(backward, "section", -1)
    grads = jnp.where(
        section_pos == last_section, fresh_grad.reshape(pb, FIRST_IN, t), moved_backward
    )

    spread_b = spread_of(inputs, up_first)
    glow_2 = lowered_grad_of(grads, down_second)
    payload = jnp.concatenate([spread_b.reshape(pb, SECOND_BLOCKS, 2 * t), glow_2], axis=2)
    arrived_b = jnp.swapaxes(to_blocks(payload), 0, 1)
    payload_b, gmix_2 = middle(arrived_b, *weights, fwd=t, bwd=t, mixed_in=mixed_s1)
    back = to_features(payload_b)
    outputs = output_of(inputs, back[:, :, :t], down_second)
    gspread_2p = back[:, :, t:].reshape(SECOND_BLOCKS, pb, 2, t)
    backward = input_grad_of(grads, gspread_2p, up_first)

    stash_both = jnp.concatenate([stash_0, stash_1], axis=2)
    gspread_both = jnp.concatenate([gspread_1p, gspread_2p], axis=3)
    spread_both = jnp.stack(
        [arrived_a[:, :, t : 3 * t], arrived_a[:, :, 4 * t : 6 * t]]
    )
    gmix_both = jnp.concatenate([gmix_1, gmix_2], axis=3)
    hidden_both = hidden_a[:, :, t:]
    glow_both = jnp.concatenate([arrived_a[:, :, 6 * t :], arrived_b[:, :, 2 * t :]], axis=2)
    lowered_both = lowered_ap[:, :, t:]
    grads_both = jnp.concatenate([first_grads, grads], axis=2)
    total_first_up = jnp.einsum(
        "pqt,rpgt->gpqr", stash_both, gspread_both, preferred_element_type=jnp.float32
    )
    total_second_up = jnp.einsum(
        "grpt,grot->grpo", spread_both, gmix_both, preferred_element_type=jnp.float32
    )
    total_first_down = jnp.einsum(
        "rot,rpt->rop", hidden_both, glow_both, preferred_element_type=jnp.float32
    )
    total_second_down = jnp.einsum(
        "rpt,pqt->prq", lowered_both, grads_both, preferred_element_type=jnp.float32
    )
    factor = 1.0 / math.sqrt(TICKS * t)
    return (
        outputs.reshape(held_input.shape),
        backward.reshape(held_grad.shape),
        (total_first_up * factor).astype(jnp.bfloat16).reshape(first_up.shape),
        (total_second_up * factor).astype(jnp.bfloat16).reshape(second_up.shape),
        (total_first_down * factor).astype(jnp.bfloat16).reshape(first_down.shape),
        (total_second_down * factor).astype(jnp.bfloat16).reshape(second_down.shape),
    )


def solution(mesh):
    return jax.shard_map(
        shards,
        mesh=mesh,
        in_specs=(
            P("section", "blk", None),
            P("blk", None),
            P("section", None, "blk", None),
            P("section", "blk", None),
            P("blk", None),
            P("section", None, "blk", None),
            P("section", None, "blk", None),
            P("section", "blk", None),
            P("section", "blk", None),
        ),
        out_specs=(
            P("section", "blk", None),
            P("section", "blk", None),
            P("section", None, "blk", None),
            P("section", None, "blk", None),
            P("section", "blk", None),
            P("section", "blk", None),
        ),
        check_vma=False,
    )
```

```python
import functools
import math

import jax
import jax.numpy as jnp
from jax import lax
from jax.experimental import pallas as pl
from jax.experimental.pallas import tpu as pltpu
from jax.sharding import PartitionSpec as P

BLOCK = 128
FIRST_BLOCKS = 128
FIRST_IN = 40
SECOND_BLOCKS = 160
TICKS = 2


def from_behind(value, axis, by):
    length = lax.axis_size(axis)
    pairs = [(i, i + by) for i in range(length) if 0 <= i + by < length]
    return lax.ppermute(value, axis, pairs)


def to_blocks(pieces):
    groups = lax.axis_size("blk")
    p_local, r_all, n = pieces.shape
    grouped = pieces.reshape(p_local, groups, r_all // groups, n).transpose(1, 2, 0, 3)
    return lax.all_to_all(grouped, "blk", split_axis=0, concat_axis=0, tiled=True)


def to_features(grouped):
    groups, r_local, p_local, n = grouped.shape
    arrived = lax.all_to_all(grouped, "blk", split_axis=0, concat_axis=0, tiled=True)
    return arrived.reshape(groups * r_local, p_local, n)


def spread_of(values, up_first):
    return jnp.einsum(
        "pqt,gpqr->prgt", values, up_first, preferred_element_type=jnp.float32
    ).astype(jnp.bfloat16)


def lowered_grad_of(grads, down_second):
    return jnp.einsum(
        "pqt,prq->prt", grads, down_second, preferred_element_type=jnp.float32
    ).astype(jnp.bfloat16)


def put(payload, r, at, value):
    rows = payload.shape[2]
    width = value.shape[1]
    for group in range(payload.shape[0]):
        payload[group, r, :, at : at + width] = value[group * rows : (group + 1) * rows].astype(
            payload.dtype
        )


def take(arrived, r, lo, hi):
    pieces = [arrived[g, r, :, lo:hi].astype(jnp.float32) for g in range(arrived.shape[0])]
    return jnp.concatenate(pieces, axis=0).astype(jnp.bfloat16)


def _middle_kernel(fwd, bwd, bwd_at, keep_at, has_mixed_in, *refs):
    refs = list(refs)
    arrived, up, up_t, down, down_t = refs[:5]
    refs = refs[5:]
    mixed_in = refs.pop(0) if has_mixed_in else None
    payload, grad_mixed = refs[0], refs[1]
    rest = refs[2:]
    hidden_out = rest.pop(0) if not has_mixed_in else None
    keep_out = rest.pop(0) if keep_at is not None else None
    for r in range(arrived.shape[1]):
        gate = jnp.dot(up_t[0, r], take(arrived, r, 0, fwd), preferred_element_type=jnp.float32)
        upper = jnp.dot(
            up_t[1, r], take(arrived, r, fwd, 2 * fwd), preferred_element_type=jnp.float32
        )
        hidden = (gate / (1.0 + jnp.exp(-gate)) * upper).astype(jnp.bfloat16)
        put(payload, r, 0, jnp.dot(down_t[r], hidden, preferred_element_type=jnp.float32))
        if hidden_out is not None:
            hidden_out[r] = hidden
        if keep_out is not None:
            keep_out[0, r] = gate[:, keep_at : keep_at + bwd]
            keep_out[1, r] = upper[:, keep_at : keep_at + bwd]
        if has_mixed_in:
            m0, m1 = mixed_in[0, r], mixed_in[1, r]
        else:
            m0, m1 = gate[:, bwd_at : bwd_at + bwd], upper[:, bwd_at : bwd_at + bwd]
        grad_hidden = jnp.dot(
            down[r], take(arrived, r, 2 * fwd, arrived.shape[3]), preferred_element_type=jnp.float32
        )
        sg = 1.0 / (1.0 + jnp.exp(-m0))
        gm0 = (grad_hidden * m1 * (sg * (1.0 + m0 * (1.0 - sg)))).astype(jnp.bfloat16)
        gm1 = (grad_hidden * m0 * sg).astype(jnp.bfloat16)
        grad_mixed[0, r] = gm0
        grad_mixed[1, r] = gm1
        put(payload, r, fwd, jnp.dot(up[0, r], gm0, preferred_element_type=jnp.float32))
        put(payload, r, fwd + bwd, jnp.dot(up[1, r], gm1, preferred_element_type=jnp.float32))


def middle(arrived, up, up_t, down, down_t, fwd, bwd, bwd_at=0, keep_at=None, mixed_in=None):
    _, rb, _, _ = arrived.shape
    pa, o = up.shape[2], up.shape[3]
    groups = lax.axis_size("blk")
    outs = [
        jax.ShapeDtypeStruct((groups, rb, pa // groups, fwd + 2 * bwd), jnp.bfloat16),
        jax.ShapeDtypeStruct((2, rb, o, bwd), jnp.bfloat16),
    ]
    if mixed_in is None:
        outs.append(jax.ShapeDtypeStruct((rb, o, fwd), jnp.bfloat16))
    if keep_at is not None:
        outs.append(jax.ShapeDtypeStruct((2, rb, o, bwd), jnp.float32))
    ins = [arrived, up, up_t, down, down_t] + ([mixed_in] if mixed_in is not None else [])
    flops = 2 * rb * o * pa * (3 * fwd + 3 * bwd)
    bytes_accessed = sum(x.size * x.dtype.itemsize for x in ins) + sum(
        math.prod(s.shape) * s.dtype.itemsize for s in outs
    )
    vmem = pltpu.MemorySpace.VMEM
    return pl.pallas_call(
        functools.partial(_middle_kernel, fwd, bwd, bwd_at, keep_at, mixed_in is not None),
        out_shape=tuple(outs),
        in_specs=[pl.BlockSpec(memory_space=vmem)] * len(ins),
        out_specs=tuple(pl.BlockSpec(memory_space=vmem) for _ in outs),
        cost_estimate=pl.CostEstimate(
            flops=flops, transcendentals=rb * o * (fwd + bwd), bytes_accessed=bytes_accessed
        ),
    )(*ins)


def output_of(values, lowered_p, down_second):
    added = jnp.einsum("rpt,prq->pqt", lowered_p, down_second, preferred_element_type=jnp.float32)
    return (values.astype(jnp.float32) + added).astype(jnp.bfloat16)


def input_grad_of(grads, grad_spread_p, up_first):
    added = jnp.einsum(
        "rpgt,gpqr->pqt", grad_spread_p, up_first, preferred_element_type=jnp.float32
    )
    return (grads.astype(jnp.float32) + added).astype(jnp.bfloat16)


def shards(
    held_input,
    fresh_input,
    stashed,
    held_grad,
    fresh_grad,
    first_up,
    second_up,
    first_down,
    second_down,
):
    pb = first_up.shape[2]
    rb = second_up.shape[2]
    t = held_input.shape[2]
    up_first = first_up[0].reshape(2, pb, FIRST_IN, SECOND_BLOCKS)
    up_second = second_up[0].reshape(2, rb, FIRST_BLOCKS, BLOCK)
    down_first = first_down[0].reshape(rb, BLOCK, FIRST_BLOCKS)
    down_second = second_down[0].reshape(pb, SECOND_BLOCKS, FIRST_IN)
    up_second_t = jnp.swapaxes(up_second, 2, 3)
    down_first_t = jnp.swapaxes(down_first, 1, 2)
    first_inputs = held_input[0].reshape(pb, FIRST_IN, t)
    first_grads = held_grad[0].reshape(pb, FIRST_IN, t)
    stash_0 = stashed[0, 0].reshape(pb, FIRST_IN, t)
    stash_1 = stashed[0, 1].reshape(pb, FIRST_IN, t)
    section_pos = lax.axis_index("section")
    last_section = lax.axis_size("section") - 1
    weights = (up_second, up_second_t, down_first, down_first_t)

    spread_a = spread_of(jnp.concatenate([first_inputs, stash_0, stash_1], axis=2), up_first)
    glow_1 = lowered_grad_of(first_grads, down_second)
    payload = jnp.concatenate([spread_a.reshape(pb, SECOND_BLOCKS, 6 * t), glow_1], axis=2)
    arrived_a = to_blocks(payload)
    payload_a, gmix_1, hidden_a, mixed_s1 = middle(
        arrived_a, *weights, fwd=3 * t, bwd=t, bwd_at=t, keep_at=2 * t
    )
    back = to_features(payload_a)
    lowered_ap = back[:, :, : 3 * t]
    gspread_1p = back[:, :, 3 * t :].reshape(SECOND_BLOCKS, pb, 2, t)
    outputs = output_of(first_inputs, lowered_ap[:, :, :t], down_second)
    backward = input_grad_of(first_grads, gspread_1p, up_first)

    moved_forward = from_behind(outputs, "section", 1)
    inputs = jnp.where(section_pos == 0, fresh_input.reshape(pb, FIRST_IN, t), moved_forward)
    moved_backward = from_behind(backward, "section", -1)
    grads = jnp.where(
        section_pos == last_section, fresh_grad.reshape(pb, FIRST_IN, t), moved_backward
    )

    spread_b = spread_of(inputs, up_first)
    glow_2 = lowered_grad_of(grads, down_second)
    payload = jnp.concatenate([spread_b.reshape(pb, SECOND_BLOCKS, 2 * t), glow_2], axis=2)
    arrived_b = to_blocks(payload)
    payload_b, gmix_2 = middle(arrived_b, *weights, fwd=t, bwd=t, mixed_in=mixed_s1)
    back = to_features(payload_b)
    outputs = output_of(inputs, back[:, :, :t], down_second)
    gspread_2p = back[:, :, t:].reshape(SECOND_BLOCKS, pb, 2, t)
    backward = input_grad_of(grads, gspread_2p, up_first)

    stash_both = jnp.concatenate([stash_0, stash_1], axis=2)
    gspread_both = jnp.concatenate([gspread_1p, gspread_2p], axis=3)
    spread_both = jnp.stack(
        [arrived_a[..., t : 3 * t], arrived_a[..., 4 * t : 6 * t]]
    )
    gmix_both = jnp.concatenate([gmix_1, gmix_2], axis=3)
    hidden_both = hidden_a[:, :, t:]
    glow_both = jnp.concatenate([arrived_a[..., 6 * t :], arrived_b[..., 2 * t :]], axis=3)
    lowered_both = lowered_ap[:, :, t:]
    grads_both = jnp.concatenate([first_grads, grads], axis=2)
    total_first_up = jnp.einsum(
        "pqt,rpgt->gpqr", stash_both, gspread_both, preferred_element_type=jnp.float32
    )
    total_second_up = jnp.einsum(
        "gsrlt,grot->grslo", spread_both, gmix_both, preferred_element_type=jnp.float32
    ).reshape(2, rb, FIRST_BLOCKS, BLOCK)
    total_first_down = jnp.einsum(
        "rot,srlt->rosl", hidden_both, glow_both, preferred_element_type=jnp.float32
    ).reshape(rb, BLOCK, FIRST_BLOCKS)
    total_second_down = jnp.einsum(
        "rpt,pqt->prq", lowered_both, grads_both, preferred_element_type=jnp.float32
    )
    factor = 1.0 / math.sqrt(TICKS * t)
    return (
        outputs.reshape(held_input.shape),
        backward.reshape(held_grad.shape),
        (total_first_up * factor).astype(jnp.bfloat16).reshape(first_up.shape),
        (total_second_up * factor).astype(jnp.bfloat16).reshape(second_up.shape),
        (total_first_down * factor).astype(jnp.bfloat16).reshape(first_down.shape),
        (total_second_down * factor).astype(jnp.bfloat16).reshape(second_down.shape),
    )


def solution(mesh):
    return jax.shard_map(
        shards,
        mesh=mesh,
        in_specs=(
            P("section", "blk", None),
            P("blk", None),
            P("section", None, "blk", None),
            P("section", "blk", None),
            P("blk", None),
            P("section", None, "blk", None),
            P("section", None, "blk", None),
            P("section", "blk", None),
            P("section", "blk", None),
        ),
        out_specs=(
            P("section", "blk", None),
            P("section", "blk", None),
            P("section", None, "blk", None),
            P("section", None, "blk", None),
            P("section", "blk", None),
            P("section", "blk", None),
        ),
        check_vma=False,
    )
```

```python
import functools
import math

import jax
import jax.numpy as jnp
from jax import lax
from jax.experimental import pallas as pl
from jax.experimental.pallas import tpu as pltpu
from jax.sharding import PartitionSpec as P

BLOCK = 128
FIRST_BLOCKS = 128
FIRST_IN = 40
SECOND_BLOCKS = 160
TICKS = 2


def from_behind(value, axis, by):
    length = lax.axis_size(axis)
    pairs = [(i, i + by) for i in range(length) if 0 <= i + by < length]
    return lax.ppermute(value, axis, pairs)


def to_blocks(pieces):
    return lax.all_to_all(pieces, "blk", split_axis=1, concat_axis=0, tiled=True)


def to_features(grouped):
    groups, r_local, p_local, n = grouped.shape
    arrived = lax.all_to_all(grouped, "blk", split_axis=0, concat_axis=0, tiled=True)
    return arrived.reshape(groups * r_local, p_local, n)


def spread_of(values, up_first):
    return jnp.einsum(
        "pqt,gpqr->prgt", values, up_first, preferred_element_type=jnp.float32
    ).astype(jnp.bfloat16)


def lowered_grad_of(grads, down_second):
    return jnp.einsum(
        "pqt,prq->prt", grads, down_second, preferred_element_type=jnp.float32
    ).astype(jnp.bfloat16)


def put(payload, r, at, value):
    rows = payload.shape[2]
    width = value.shape[1]
    for group in range(payload.shape[0]):
        payload[group, r, :, at : at + width] = value[group * rows : (group + 1) * rows].astype(
            payload.dtype
        )


def _forward_kernel(width, gate_at, up_at, *refs):
    arrived, up_t, down_t, lowered, hidden_out, keep_out = refs
    for r in range(arrived.shape[0]):
        gate = jnp.dot(
            up_t[0, r], arrived[r, :, gate_at : gate_at + width], preferred_element_type=jnp.float32
        )
        upper = jnp.dot(
            up_t[1, r], arrived[r, :, up_at : up_at + width], preferred_element_type=jnp.float32
        )
        hidden = (gate / (1.0 + jnp.exp(-gate)) * upper).astype(jnp.bfloat16)
        put(lowered, r, 0, jnp.dot(down_t[r], hidden, preferred_element_type=jnp.float32))
        hidden_out[r] = hidden
        keep_out[0, r] = gate
        keep_out[1, r] = upper


def forward_only(arrived, up_t, down_t, width, gate_at, up_at):
    rb, pa, _ = arrived.shape
    o = up_t.shape[2]
    groups = lax.axis_size("blk")
    outs = (
        jax.ShapeDtypeStruct((groups, rb, pa // groups, width), jnp.bfloat16),
        jax.ShapeDtypeStruct((rb, o, width), jnp.bfloat16),
        jax.ShapeDtypeStruct((2, rb, o, width), jnp.float32),
    )
    vmem = pltpu.MemorySpace.VMEM
    return pl.pallas_call(
        functools.partial(_forward_kernel, width, gate_at, up_at),
        out_shape=outs,
        in_specs=[pl.BlockSpec(memory_space=vmem)] * 3,
        out_specs=tuple(pl.BlockSpec(memory_space=vmem) for _ in outs),
        cost_estimate=pl.CostEstimate(
            flops=2 * rb * o * pa * 3 * width,
            transcendentals=rb * o * width,
            bytes_accessed=arrived.size * 2 + up_t.size * 2 + down_t.size * 2 + rb * o * width * 14,
        ),
    )(arrived, up_t, down_t)


def _middle_kernel(fwd, bwd, bwd_at, keep_at, has_mixed_in, cols, has_extra, *refs):
    refs = list(refs)
    arrived, up, up_t, down, down_t = refs[:5]
    refs = refs[5:]
    mixed_in = refs.pop(0) if has_mixed_in else None
    extra = refs.pop(0) if has_extra else None
    payload, grad_mixed = refs[0], refs[1]
    rest = refs[2:]
    hidden_out = rest.pop(0) if not has_mixed_in else None
    keep_out = rest.pop(0) if keep_at is not None else None
    gate_at, up_at, grad_at = cols
    for r in range(arrived.shape[0]):
        gate = jnp.dot(
            up_t[0, r], arrived[r, :, gate_at : gate_at + fwd], preferred_element_type=jnp.float32
        )
        upper = jnp.dot(
            up_t[1, r], arrived[r, :, up_at : up_at + fwd], preferred_element_type=jnp.float32
        )
        hidden = (gate / (1.0 + jnp.exp(-gate)) * upper).astype(jnp.bfloat16)
        put(payload, r, 0, jnp.dot(down_t[r], hidden, preferred_element_type=jnp.float32))
        if hidden_out is not None:
            hidden_out[r] = hidden
        if keep_out is not None:
            keep_out[0, r] = gate[:, keep_at : keep_at + bwd]
            keep_out[1, r] = upper[:, keep_at : keep_at + bwd]
        if has_mixed_in:
            m0, m1 = mixed_in[0, r], mixed_in[1, r]
        else:
            m0, m1 = gate[:, bwd_at : bwd_at + bwd], upper[:, bwd_at : bwd_at + bwd]
        grad_hidden = jnp.dot(
            down[r], arrived[r, :, grad_at : grad_at + bwd], preferred_element_type=jnp.float32
        )
        sg = 1.0 / (1.0 + jnp.exp(-m0))
        gm0 = (grad_hidden * m1 * (sg * (1.0 + m0 * (1.0 - sg)))).astype(jnp.bfloat16)
        gm1 = (grad_hidden * m0 * sg).astype(jnp.bfloat16)
        grad_mixed[0, r] = gm0
        grad_mixed[1, r] = gm1
        put(payload, r, fwd, jnp.dot(up[0, r], gm0, preferred_element_type=jnp.float32))
        put(payload, r, fwd + bwd, jnp.dot(up[1, r], gm1, preferred_element_type=jnp.float32))
        if extra is not None:
            payload[:, r, :, fwd + 2 * bwd :] = extra[:, r]


def middle(
    arrived, up, up_t, down, down_t, fwd, bwd, cols, bwd_at=0, keep_at=None, mixed_in=None, extra=None
):
    rb, pa, _ = arrived.shape
    o = up.shape[3]
    groups = lax.axis_size("blk")
    outs = [
        jax.ShapeDtypeStruct(
            (groups, rb, pa // groups, fwd + 2 * bwd + (0 if extra is None else extra.shape[3])),
            jnp.bfloat16,
        ),
        jax.ShapeDtypeStruct((2, rb, o, bwd), jnp.bfloat16),
    ]
    if mixed_in is None:
        outs.append(jax.ShapeDtypeStruct((rb, o, fwd), jnp.bfloat16))
    if keep_at is not None:
        outs.append(jax.ShapeDtypeStruct((2, rb, o, bwd), jnp.float32))
    ins = [arrived, up, up_t, down, down_t] + ([mixed_in] if mixed_in is not None else [])
    ins += [extra] if extra is not None else []
    flops = 2 * rb * o * pa * (3 * fwd + 3 * bwd)
    bytes_accessed = sum(x.size * x.dtype.itemsize for x in ins) + sum(
        math.prod(s.shape) * s.dtype.itemsize for s in outs
    )
    vmem = pltpu.MemorySpace.VMEM
    return pl.pallas_call(
        functools.partial(
            _middle_kernel, fwd, bwd, bwd_at, keep_at, mixed_in is not None, cols, extra is not None
        ),
        out_shape=tuple(outs),
        in_specs=[pl.BlockSpec(memory_space=vmem)] * len(ins),
        out_specs=tuple(pl.BlockSpec(memory_space=vmem) for _ in outs),
        cost_estimate=pl.CostEstimate(
            flops=flops, transcendentals=rb * o * (fwd + bwd), bytes_accessed=bytes_accessed
        ),
    )(*ins)


def output_of(values, lowered_p, down_second):
    added = jnp.einsum("rpt,prq->pqt", lowered_p, down_second, preferred_element_type=jnp.float32)
    return (values.astype(jnp.float32) + added).astype(jnp.bfloat16)


def input_grad_of(grads, grad_spread_p, up_first):
    added = jnp.einsum(
        "rpgt,gpqr->pqt", grad_spread_p, up_first, preferred_element_type=jnp.float32
    )
    return (grads.astype(jnp.float32) + added).astype(jnp.bfloat16)


def shards(
    held_input,
    fresh_input,
    stashed,
    held_grad,
    fresh_grad,
    first_up,
    second_up,
    first_down,
    second_down,
):
    pb = first_up.shape[2]
    rb = second_up.shape[2]
    t = held_input.shape[2]
    up_first = first_up[0].reshape(2, pb, FIRST_IN, SECOND_BLOCKS)
    up_second = second_up[0].reshape(2, rb, FIRST_BLOCKS, BLOCK)
    down_first = first_down[0].reshape(rb, BLOCK, FIRST_BLOCKS)
    down_second = second_down[0].reshape(pb, SECOND_BLOCKS, FIRST_IN)
    up_second_t = jnp.swapaxes(up_second, 2, 3)
    down_first_t = jnp.swapaxes(down_first, 1, 2)
    first_inputs = held_input[0].reshape(pb, FIRST_IN, t)
    first_grads = held_grad[0].reshape(pb, FIRST_IN, t)
    stash_0 = stashed[0, 0].reshape(pb, FIRST_IN, t)
    stash_1 = stashed[0, 1].reshape(pb, FIRST_IN, t)
    section_pos = lax.axis_index("section")
    last_section = lax.axis_size("section") - 1
    weights = (up_second, up_second_t, down_first, down_first_t)

    spread_a = spread_of(jnp.concatenate([first_inputs, stash_0, stash_1], axis=2), up_first)
    glow_1 = lowered_grad_of(first_grads, down_second)
    payload = jnp.concatenate([spread_a.reshape(pb, SECOND_BLOCKS, 6 * t), glow_1], axis=2)
    arrived_a = jnp.swapaxes(to_blocks(payload), 0, 1)
    payload_a, gmix_1, hidden_a = middle(
        arrived_a, *weights, fwd=2 * t, bwd=t, cols=(0, 3 * t, 6 * t), bwd_at=t
    )
    back = to_features(payload_a)
    lowered_ap = back[:, :, : 2 * t]
    gspread_1p = back[:, :, 2 * t :].reshape(SECOND_BLOCKS, pb, 2, t)
    lowered_s1, hidden_s1, mixed_s1 = forward_only(
        arrived_a, up_second_t, down_first_t, t, 2 * t, 5 * t
    )
    outputs = output_of(first_inputs, lowered_ap[:, :, :t], down_second)
    backward = input_grad_of(first_grads, gspread_1p, up_first)

    moved_forward = from_behind(outputs, "section", 1)
    inputs = jnp.where(section_pos == 0, fresh_input.reshape(pb, FIRST_IN, t), moved_forward)
    moved_backward = from_behind(backward, "section", -1)
    grads = jnp.where(
        section_pos == last_section, fresh_grad.reshape(pb, FIRST_IN, t), moved_backward
    )

    spread_b = spread_of(inputs, up_first)
    glow_2 = lowered_grad_of(grads, down_second)
    payload = jnp.concatenate([spread_b.reshape(pb, SECOND_BLOCKS, 2 * t), glow_2], axis=2)
    arrived_b = jnp.swapaxes(to_blocks(payload), 0, 1)
    payload_b, gmix_2 = middle(
        arrived_b, *weights, fwd=t, bwd=t, cols=(0, t, 2 * t), mixed_in=mixed_s1, extra=lowered_s1
    )
    back = to_features(payload_b)
    outputs = output_of(inputs, back[:, :, :t], down_second)
    gspread_2p = back[:, :, t : 3 * t].reshape(SECOND_BLOCKS, pb, 2, t)
    lowered_s1p = back[:, :, 3 * t :]
    backward = input_grad_of(grads, gspread_2p, up_first)

    stash_both = jnp.concatenate([stash_0, stash_1], axis=2)
    gspread_both = jnp.concatenate([gspread_1p, gspread_2p], axis=3)
    spread_both = jnp.stack(
        [arrived_a[:, :, t : 3 * t], arrived_a[:, :, 4 * t : 6 * t]]
    )
    gmix_both = jnp.concatenate([gmix_1, gmix_2], axis=3)
    hidden_both = jnp.concatenate([hidden_a[:, :, t:], hidden_s1], axis=2)
    glow_both = jnp.concatenate([arrived_a[:, :, 6 * t :], arrived_b[:, :, 2 * t :]], axis=2)
    lowered_both = jnp.concatenate([lowered_ap[:, :, t:], lowered_s1p], axis=2)
    grads_both = jnp.concatenate([first_grads, grads], axis=2)
    total_first_up = jnp.einsum(
        "pqt,rpgt->gpqr", stash_both, gspread_both, preferred_element_type=jnp.float32
    )
    total_second_up = jnp.einsum(
        "grpt,grot->grpo", spread_both, gmix_both, preferred_element_type=jnp.float32
    )
    total_first_down = jnp.einsum(
        "rot,rpt->rop", hidden_both, glow_both, preferred_element_type=jnp.float32
    )
    total_second_down = jnp.einsum(
        "rpt,pqt->prq", lowered_both, grads_both, preferred_element_type=jnp.float32
    )
    factor = 1.0 / math.sqrt(TICKS * t)
    return (
        outputs.reshape(held_input.shape),
        backward.reshape(held_grad.shape),
        (total_first_up * factor).astype(jnp.bfloat16).reshape(first_up.shape),
        (total_second_up * factor).astype(jnp.bfloat16).reshape(second_up.shape),
        (total_first_down * factor).astype(jnp.bfloat16).reshape(first_down.shape),
        (total_second_down * factor).astype(jnp.bfloat16).reshape(second_down.shape),
    )


def solution(mesh):
    return jax.shard_map(
        shards,
        mesh=mesh,
        in_specs=(
            P("section", "blk", None),
            P("blk", None),
            P("section", None, "blk", None),
            P("section", "blk", None),
            P("blk", None),
            P("section", None, "blk", None),
            P("section", None, "blk", None),
            P("section", "blk", None),
            P("section", "blk", None),
        ),
        out_specs=(
            P("section", "blk", None),
            P("section", "blk", None),
            P("section", None, "blk", None),
            P("section", None, "blk", None),
            P("section", "blk", None),
            P("section", "blk", None),
        ),
        check_vma=False,
    )
```

```python
import functools
import math

import jax
import jax.numpy as jnp
from jax import lax
from jax.experimental import pallas as pl
from jax.experimental.pallas import tpu as pltpu
from jax.sharding import PartitionSpec as P

BLOCK = 128
FIRST_BLOCKS = 128
FIRST_IN = 40
SECOND_BLOCKS = 160
TICKS = 2


def from_behind(value, axis, by):
    length = lax.axis_size(axis)
    pairs = [(i, i + by) for i in range(length) if 0 <= i + by < length]
    return lax.ppermute(value, axis, pairs)


def to_blocks(pieces):
    return lax.all_to_all(pieces, "blk", split_axis=1, concat_axis=0, tiled=True)


def to_features(grouped):
    groups, r_local, p_local, n = grouped.shape
    arrived = lax.all_to_all(grouped, "blk", split_axis=0, concat_axis=0, tiled=True)
    return arrived.reshape(groups * r_local, p_local, n)


def spread_of(values, up_first):
    return jnp.einsum(
        "pqt,gpqr->prgt", values, up_first, preferred_element_type=jnp.float32
    ).astype(jnp.bfloat16)


def lowered_grad_of(grads, down_second):
    return jnp.einsum(
        "pqt,prq->prt", grads, down_second, preferred_element_type=jnp.float32
    ).astype(jnp.bfloat16)


def put(payload, r, at, value):
    rows = payload.shape[2]
    width = value.shape[1]
    for group in range(payload.shape[0]):
        payload[group, r, :, at : at + width] = value[group * rows : (group + 1) * rows].astype(
            payload.dtype
        )


def _middle_kernel(fwd, bwd, bwd_at, keep_at, has_mixed_in, *refs):
    refs = list(refs)
    arrived, up, up_t, down, down_t = refs[:5]
    refs = refs[5:]
    mixed_in = refs.pop(0) if has_mixed_in else None
    payload, grad_mixed = refs[0], refs[1]
    rest = refs[2:]
    hidden_out = rest.pop(0) if not has_mixed_in else None
    keep_out = rest.pop(0) if keep_at is not None else None
    for r in range(arrived.shape[0]):
        gate = jnp.dot(up_t[0, r], arrived[r, :, :fwd], preferred_element_type=jnp.float32)
        upper = jnp.dot(
            up_t[1, r], arrived[r, :, fwd : 2 * fwd], preferred_element_type=jnp.float32
        )
        hidden = (gate / (1.0 + jnp.exp(-gate)) * upper).astype(jnp.bfloat16)
        put(payload, r, 0, jnp.dot(down_t[r], hidden, preferred_element_type=jnp.float32))
        if hidden_out is not None:
            hidden_out[r] = hidden[:, bwd_at:]
        if keep_out is not None:
            keep_out[0, r] = gate[:, keep_at : keep_at + bwd]
            keep_out[1, r] = upper[:, keep_at : keep_at + bwd]
        if has_mixed_in:
            m0, m1 = mixed_in[0, r], mixed_in[1, r]
        else:
            m0, m1 = gate[:, bwd_at : bwd_at + bwd], upper[:, bwd_at : bwd_at + bwd]
        grad_hidden = jnp.dot(
            down[r], arrived[r, :, 2 * fwd :], preferred_element_type=jnp.float32
        )
        sg = 1.0 / (1.0 + jnp.exp(-m0))
        gm0 = (grad_hidden * m1 * (sg * (1.0 + m0 * (1.0 - sg)))).astype(jnp.bfloat16)
        gm1 = (grad_hidden * m0 * sg).astype(jnp.bfloat16)
        grad_mixed[0, r] = gm0
        grad_mixed[1, r] = gm1
        put(payload, r, fwd, jnp.dot(up[0, r], gm0, preferred_element_type=jnp.float32))
        put(payload, r, fwd + bwd, jnp.dot(up[1, r], gm1, preferred_element_type=jnp.float32))


def middle(arrived, up, up_t, down, down_t, fwd, bwd, bwd_at=0, keep_at=None, mixed_in=None):
    rb, pa, _ = arrived.shape
    o = up.shape[3]
    groups = lax.axis_size("blk")
    outs = [
        jax.ShapeDtypeStruct((groups, rb, pa // groups, fwd + 2 * bwd), jnp.bfloat16),
        jax.ShapeDtypeStruct((2, rb, o, bwd), jnp.bfloat16),
    ]
    if mixed_in is None:
        outs.append(jax.ShapeDtypeStruct((rb, o, fwd - bwd_at), jnp.bfloat16))
    if keep_at is not None:
        outs.append(jax.ShapeDtypeStruct((2, rb, o, bwd), jnp.float32))
    ins = [arrived, up, up_t, down, down_t] + ([mixed_in] if mixed_in is not None else [])
    flops = 2 * rb * o * pa * (3 * fwd + 3 * bwd)
    bytes_accessed = sum(x.size * x.dtype.itemsize for x in ins) + sum(
        math.prod(s.shape) * s.dtype.itemsize for s in outs
    )
    vmem = pltpu.MemorySpace.VMEM
    return pl.pallas_call(
        functools.partial(_middle_kernel, fwd, bwd, bwd_at, keep_at, mixed_in is not None),
        out_shape=tuple(outs),
        in_specs=[pl.BlockSpec(memory_space=vmem)] * len(ins),
        out_specs=tuple(pl.BlockSpec(memory_space=vmem) for _ in outs),
        cost_estimate=pl.CostEstimate(
            flops=flops, transcendentals=rb * o * (fwd + bwd), bytes_accessed=bytes_accessed
        ),
    )(*ins)


def output_of(values, lowered_p, down_second):
    added = jnp.einsum("rpt,prq->pqt", lowered_p, down_second, preferred_element_type=jnp.float32)
    return (values.astype(jnp.float32) + added).astype(jnp.bfloat16)


def input_grad_of(grads, grad_spread_p, up_first):
    added = jnp.einsum(
        "rpgt,gpqr->pqt", grad_spread_p, up_first, preferred_element_type=jnp.float32
    )
    return (grads.astype(jnp.float32) + added).astype(jnp.bfloat16)


def shards(
    held_input,
    fresh_input,
    stashed,
    held_grad,
    fresh_grad,
    first_up,
    second_up,
    first_down,
    second_down,
):
    pb = first_up.shape[2]
    rb = second_up.shape[2]
    t = held_input.shape[2]
    up_first = first_up[0].reshape(2, pb, FIRST_IN, SECOND_BLOCKS)
    up_second = second_up[0].reshape(2, rb, FIRST_BLOCKS, BLOCK)
    down_first = first_down[0].reshape(rb, BLOCK, FIRST_BLOCKS)
    down_second = second_down[0].reshape(pb, SECOND_BLOCKS, FIRST_IN)
    up_second_t = jnp.swapaxes(up_second, 2, 3)
    down_first_t = jnp.swapaxes(down_first, 1, 2)
    first_inputs = held_input[0].reshape(pb, FIRST_IN, t)
    first_grads = held_grad[0].reshape(pb, FIRST_IN, t)
    stash_0 = stashed[0, 0].reshape(pb, FIRST_IN, t)
    stash_1 = stashed[0, 1].reshape(pb, FIRST_IN, t)
    section_pos = lax.axis_index("section")
    last_section = lax.axis_size("section") - 1
    weights = (up_second, up_second_t, down_first, down_first_t)

    spread_a = spread_of(jnp.concatenate([first_inputs, stash_0, stash_1], axis=2), up_first)
    glow_1 = lowered_grad_of(first_grads, down_second)
    payload = jnp.concatenate([spread_a.reshape(pb, SECOND_BLOCKS, 6 * t), glow_1], axis=2)
    arrived_a = jnp.swapaxes(to_blocks(payload), 0, 1)
    payload_a, gmix_1, hidden_a, mixed_s1 = middle(
        arrived_a, *weights, fwd=3 * t, bwd=t, bwd_at=t, keep_at=2 * t
    )
    back = to_features(payload_a)
    lowered_ap = back[:, :, : 3 * t]
    gspread_1p = back[:, :, 3 * t :].reshape(SECOND_BLOCKS, pb, 2, t)
    outputs = output_of(first_inputs, lowered_ap[:, :, :t], down_second)
    backward = input_grad_of(first_grads, gspread_1p, up_first)

    moved_forward = from_behind(outputs, "section", 1)
    inputs = jnp.where(section_pos == 0, fresh_input.reshape(pb, FIRST_IN, t), moved_forward)
    moved_backward = from_behind(backward, "section", -1)
    grads = jnp.where(
        section_pos == last_section, fresh_grad.reshape(pb, FIRST_IN, t), moved_backward
    )

    spread_b = spread_of(inputs, up_first)
    glow_2 = lowered_grad_of(grads, down_second)
    payload = jnp.concatenate([spread_b.reshape(pb, SECOND_BLOCKS, 2 * t), glow_2], axis=2)
    arrived_b = jnp.swapaxes(to_blocks(payload), 0, 1)
    payload_b, gmix_2 = middle(arrived_b, *weights, fwd=t, bwd=t, mixed_in=mixed_s1)
    back = to_features(payload_b)
    outputs = output_of(inputs, back[:, :, :t], down_second)
    gspread_2p = back[:, :, t:].reshape(SECOND_BLOCKS, pb, 2, t)
    backward = input_grad_of(grads, gspread_2p, up_first)

    stash_both = jnp.concatenate([stash_0, stash_1], axis=2)
    gspread_both = jnp.concatenate([gspread_1p, gspread_2p], axis=3)
    spread_both = jnp.stack(
        [arrived_a[:, :, t : 3 * t], arrived_a[:, :, 4 * t : 6 * t]]
    )
    gmix_both = jnp.concatenate([gmix_1, gmix_2], axis=3)
    hidden_both = hidden_a
    glow_both = jnp.concatenate([arrived_a[:, :, 6 * t :], arrived_b[:, :, 2 * t :]], axis=2)
    lowered_both = lowered_ap[:, :, t:]
    grads_both = jnp.concatenate([first_grads, grads], axis=2)
    total_first_up = jnp.einsum(
        "pqt,rpgt->gpqr", stash_both, gspread_both, preferred_element_type=jnp.float32
    )
    total_second_up = jnp.einsum(
        "grpt,grot->grpo", spread_both, gmix_both, preferred_element_type=jnp.float32
    )
    total_first_down = jnp.einsum(
        "rot,rpt->rop", hidden_both, glow_both, preferred_element_type=jnp.float32
    )
    total_second_down = jnp.einsum(
        "rpt,pqt->prq", lowered_both, grads_both, preferred_element_type=jnp.float32
    )
    factor = 1.0 / math.sqrt(TICKS * t)
    return (
        outputs.reshape(held_input.shape),
        backward.reshape(held_grad.shape),
        (total_first_up * factor).astype(jnp.bfloat16).reshape(first_up.shape),
        (total_second_up * factor).astype(jnp.bfloat16).reshape(second_up.shape),
        (total_first_down * factor).astype(jnp.bfloat16).reshape(first_down.shape),
        (total_second_down * factor).astype(jnp.bfloat16).reshape(second_down.shape),
    )


def solution(mesh):
    return jax.shard_map(
        shards,
        mesh=mesh,
        in_specs=(
            P("section", "blk", None),
            P("blk", None),
            P("section", None, "blk", None),
            P("section", "blk", None),
            P("blk", None),
            P("section", None, "blk", None),
            P("section", None, "blk", None),
            P("section", "blk", None),
            P("section", "blk", None),
        ),
        out_specs=(
            P("section", "blk", None),
            P("section", "blk", None),
            P("section", None, "blk", None),
            P("section", None, "blk", None),
            P("section", "blk", None),
            P("section", "blk", None),
        ),
        check_vma=False,
    )
```
